512 devices in a mesh: box: 128 (over x, y_lo, z), exc: 4 (over y_hi, core).
Axes of the slice: x: 4, y: 8 (y_hi: 2, y_lo: 4; y = y_hi * 4 + y_lo), z: 8, core: 2. Of those that a mesh axis runs over, the one named last changes fastest.
Arguments:
- incident: bfloat16 [2, 8, 512, 512], P(None, 'exc', 'box'), may hold values from -7 to 7
- contrast: int32 [512, 512], P('box'), may hold values from 1 to 16
- box_pos: int32 [512], replicated, may hold values from 0 to 3, as said below
- directions: float32 [3, 512], P(None, 'box'), may hold values from -1 to 1, as said below
- enc_table: bfloat16 [2, 512, 512], replicated, may hold values from -0.25 to 0.25
- dec_table: bfloat16 [2, 512, 512], replicated, may hold values from -0.25 to 0.25
Outputs:
- scattered_one: bfloat16 [2, 8, 512, 512], P(None, 'exc', 'box')
- scattered_two: bfloat16 [2, 8, 512, 512], P(None, 'exc', 'box')
- series_ratio: float32 [512], P('box')
The draws below stay inside these ranges and needn't reach their ends.
Inputs may be any that keep to these rules, and one draw needn't show every extreme that they name: `box_pos`: entries 4 m to 4 m + 3 hold each number from 0 to 3 once. `directions`: each column is a unit vector.
All inputs are finite; a program needn't handle non-finite values.
Results may differ from the reference program's by a relative error of at most 0.0053.
Values may be sent and summed in bfloat16 or wider, within the bound.
No kernel may reach another device: no remote copies, remote signals or barrier semaphores. Data moves between devices by JAX's collectives and lax.ppermute only.
A program may use at most 128 MiB of HBM per device.

```python
import math
import jax
import jax.numpy as jnp
from jax import lax

BSIDE = 8
CY = 2
CZ = 2
K = 512
V = 512
BOX_DEV = 4
BOXES = 512
EXC = 8


def draw_incident(key, part):
    ramp = jnp.arange(EXC, dtype=jnp.float32) / max(EXC - 1, 1)
    values = jnp.clip(jax.random.normal(key, (2, EXC, BOXES, V), jnp.float32), -4.0, 4.0)
    amplitude = 3.0 ** (ramp - 0.5)
    return (values * amplitude[None, :, None, None]).astype(jnp.bfloat16)


def permute_slab(subkey):
    return jax.random.permutation(subkey, CY * CZ)


def draw_box_pos(key, part):
    slab_count = BOXES // (CY * CZ)
    key_list = jax.random.split(key, slab_count)
    return jax.vmap(permute_slab)(key_list).reshape(BOXES).astype(jnp.int32)


def draw_directions(key, part):
    first_key, second_key = jax.random.split(jax.random.fold_in(key, 7))
    height = jax.random.uniform(first_key, (K,), jnp.float32, -1.0, 1.0)
    azimuth = jax.random.uniform(second_key, (K,), jnp.float32, -math.pi, math.pi)
    beside_all = jnp.sqrt(jnp.maximum(1.0 - height * height, 0.0))
    return jnp.stack([beside_all * jnp.cos(azimuth), beside_all * jnp.sin(azimuth), height]).astype(jnp.float32)


def touch_ends(array, own_key, low, largest):
    place = [jax.random.randint(jax.random.fold_in(own_key, axis), (), 0, length) for axis, length in enumerate(array.shape)]
    widest = array.shape.index(max(array.shape))
    neighbour = place[:widest] + [(place[widest] + 1) % array.shape[widest]] + place[widest + 1:]
    return array.at[tuple(place)].set(low).at[tuple(neighbour)].set(largest)


def normal_values(stream_key, dims, deviation, bound, held_as=jnp.bfloat16):
    return jnp.clip(deviation * jax.random.normal(stream_key, dims, jnp.float32), -bound, bound).astype(held_as)


def setup_inputs(seed: int = 0) -> dict:
    streams_of = jax.random.split(jax.random.key(seed), 7)
    return {
        "incident": draw_incident(jax.random.fold_in(streams_of[6], 71), 0),
        "contrast": touch_ends(jax.random.randint(streams_of[1], (BOXES, V), 1, 17), jax.random.fold_in(streams_of[1], 1), 1, 16).astype(jnp.int32),
        "box_pos": draw_box_pos(jax.random.fold_in(streams_of[6], 71), 0),
        "directions": draw_directions(jax.random.fold_in(streams_of[6], 71), 0),
        "enc_table": normal_values(streams_of[4], (2, K, V), V ** -0.5, 0.25),
        "dec_table": normal_values(streams_of[5], (2, V, K), K ** -0.5, 0.25),
    }


wave_number = 0.8
near_scale = 0.1
self_value = 1.0
far_scale = 0.25
chi_step = 0.0625
epsilon = 1e-06

def voxel_axes():
    voxel_index = jnp.arange(BSIDE ** 3, dtype=jnp.int32)
    return (voxel_index // (BSIDE * BSIDE), voxel_index // BSIDE % BSIDE, voxel_index % BSIDE)

def green_block(offset):
    coords = voxel_axes()
    square = jnp.zeros((BSIDE ** 3, BSIDE ** 3), jnp.int32)
    for dimension in range(3):
        differ = coords[dimension][:, None] - coords[dimension][None, :] - BSIDE * offset[dimension]
        square = square + differ * differ
    square = square.astype(jnp.float32)
    radius = jnp.sqrt(jnp.maximum(square, 1.0))
    inside = square < 0.5
    real_part = jnp.where(inside, self_value, near_scale * jnp.cos(wave_number * radius) / radius)
    imag_part = jnp.where(inside, 0.0, near_scale * jnp.sin(wave_number * radius) / radius)
    return jnp.stack([real_part, imag_part]).astype(jnp.bfloat16)

def box_coords(box_pos):
    box_count = box_pos.shape[0]
    slab_coord = (jnp.arange(box_count, dtype=jnp.int32) // (CY * CZ)).astype(jnp.float32)
    row_coord = (box_pos // CZ).astype(jnp.float32)
    col_coord = (box_pos % CZ).astype(jnp.float32)
    return (slab_coord, row_coord, col_coord)

def translator(column, coords):
    slab_gap = coords[0][:, None] - coords[0][None, :]
    row_gap = coords[1][:, None] - coords[1][None, :]
    col_gap = coords[2][:, None] - coords[2][None, :]
    square = slab_gap * slab_gap + row_gap * row_gap + col_gap * col_gap
    nearby = jnp.maximum(jnp.maximum(jnp.abs(slab_gap), jnp.abs(row_gap)), jnp.abs(col_gap)) < 1.5
    radius = jnp.sqrt(jnp.maximum(square, 1.0))
    kappa = wave_number * BSIDE
    argument = kappa * radius
    inverse = 1.0 / argument
    cosine = (column[0] * slab_gap + column[1] * row_gap + column[2] * col_gap) / radius
    prev_re, prev_im = (inverse, jnp.zeros_like(inverse))
    now_re, now_im = (jnp.zeros_like(inverse), -inverse)
    leg_prev, leg_now = (jnp.ones_like(inverse), jnp.ones_like(inverse))
    total_re = jnp.zeros_like(inverse)
    total_im = jnp.zeros_like(inverse)
    for order in range(4):
        if order == 0:
            legendre = jnp.ones_like(inverse)
        elif order == 1:
            legendre = cosine
        else:
            legendre = ((2 * order - 1) * cosine * leg_now - (order - 1) * leg_prev) / order
        leg_prev, leg_now = (leg_now, legendre)
        weight = (2.0 * order + 1.0) * legendre
        rot = order % 4
        if rot == 0:
            term_re, term_im = (now_re, now_im)
        elif rot == 1:
            term_re, term_im = (-now_im, now_re)
        elif rot == 2:
            term_re, term_im = (-now_re, -now_im)
        else:
            term_re, term_im = (now_im, -now_re)
        total_re = total_re + weight * term_re
        total_im = total_im + weight * term_im
        next_re = (2.0 * order + 1.0) * inverse * now_re - prev_re
        next_im = (2.0 * order + 1.0) * inverse * now_im - prev_im
        prev_re, prev_im = (now_re, now_im)
        now_re, now_im = (next_re, next_im)
    wave_re = jnp.cos(argument)
    wave_im = jnp.sin(argument)
    factor = jnp.where(nearby, 0.0, far_scale * kappa / 16.0)
    real_part = factor * (total_re * wave_re - total_im * wave_im)
    imag_part = factor * (total_re * wave_im + total_im * wave_re)
    return jnp.stack([real_part, imag_part]).astype(jnp.bfloat16)

def near_reference(sources, slots):
    slab_count = BOXES // BOX_DEV
    grid = jnp.zeros_like(sources).at[:, :, slots, :].set(sources)
    grid = grid.astype(jnp.float32).reshape(2, EXC, slab_count, CY, CZ, V)
    padded = jnp.pad(grid, ((0, 0), (0, 0), (1, 1), (0, 0), (0, 0), (0, 0)))
    accumulated = jnp.zeros((2, EXC, slab_count, CY, CZ, V), jnp.float32)
    for shift_x in (-1, 0, 1):
        for shift_y in (-1, 0, 1):
            for shift_z in (-1, 0, 1):
                row_low = max(0, -shift_y)
                row_high = CY - max(0, shift_y)
                col_low = max(0, -shift_z)
                col_high = CZ - max(0, shift_z)
                if row_high <= row_low or col_high <= col_low:
                    continue
                block = green_block((shift_x, shift_y, shift_z)).astype(jnp.float32)
                piece = padded[:, :, 1 + shift_x:1 + shift_x + slab_count, row_low + shift_y:row_high + shift_y, col_low + shift_z:col_high + shift_z, :]
                real_prod = jnp.einsum('xesyzj,ij->xesyzi', piece, block[0], precision=lax.Precision.HIGHEST)
                imag_prod = jnp.einsum('xesyzj,ij->xesyzi', piece, block[1], precision=lax.Precision.HIGHEST)
                update = jnp.stack([real_prod[0] - imag_prod[1], imag_prod[0] + real_prod[1]])
                accumulated = accumulated.at[:, :, :, row_low:row_high, col_low:col_high, :].add(update)
    return accumulated.reshape(2, EXC, BOXES, V)[:, :, slots, :]

def reference(incident, contrast, box_pos, directions, enc_table, dec_table):
    contrast_real = contrast.astype(jnp.float32) * chi_step
    coords = box_coords(box_pos)
    slots = jnp.arange(BOXES, dtype=jnp.int32) // BOX_DEV * BOX_DEV + box_pos
    enc_float = enc_table.astype(jnp.float32)
    dec_float = dec_table.astype(jnp.float32)
    fields = incident
    outputs = []
    for term_index in range(2):
        sources = (contrast_real[None, None] * fields.astype(jnp.float32)).astype(jnp.bfloat16)
        near_part = near_reference(sources, slots)
        source_float = sources.astype(jnp.float32)
        real_prod = jnp.einsum('kv,xebv->kxeb', enc_float[0], source_float, precision=lax.Precision.HIGHEST)
        imag_prod = jnp.einsum('kv,xebv->kxeb', enc_float[1], source_float, precision=lax.Precision.HIGHEST)
        encoded = jnp.stack([real_prod[:, 0] - imag_prod[:, 1], imag_prod[:, 0] + real_prod[:, 1]], axis=1).astype(jnp.bfloat16)

        def one_direction(packed):
            column, coefficients = packed
            block = translator(column, coords).astype(jnp.float32)
            values = coefficients.astype(jnp.float32)
            real_part = jnp.einsum('ts,xes->xet', block[0], values, precision=lax.Precision.HIGHEST)
            imag_part = jnp.einsum('ts,xes->xet', block[1], values, precision=lax.Precision.HIGHEST)
            return jnp.stack([real_part[0] - imag_part[1], imag_part[0] + real_part[1]]).astype(jnp.bfloat16)
        translated = lax.map(one_direction, (jnp.transpose(directions), encoded)).astype(jnp.float32)
        real_back = jnp.einsum('vk,kxeb->xebv', dec_float[0], translated, precision=lax.Precision.HIGHEST)
        imag_back = jnp.einsum('vk,kxeb->xebv', dec_float[1], translated, precision=lax.Precision.HIGHEST)
        far_part = jnp.stack([real_back[0] - imag_back[1], imag_back[0] + real_back[1]])
        fields = (near_part + far_part).astype(jnp.bfloat16)
        outputs.append(fields)
    first_mean = lax.optimization_barrier(jnp.mean(jnp.square(outputs[0].astype(jnp.float32)), axis=(0, 1, 3)))
    second_mean = lax.optimization_barrier(jnp.mean(jnp.square(outputs[1].astype(jnp.float32)), axis=(0, 1, 3)))
    series_ratio = jnp.sqrt(second_mean / (first_mean + epsilon))
    return (outputs[0], outputs[1], series_ratio)
```

```python
import numpy as np
import jax
import jax.numpy as jnp
from jax import lax
from jax.sharding import PartitionSpec as P

BSIDE = 8
CY = 2
CZ = 2
V = 512


wave_number = 0.8
near_scale = 0.1
self_value = 1.0
far_scale = 0.25
chi_step = 0.0625
epsilon = 1e-06


def padded(block, sides, width):
    for axis, dim in sides:
        count = lax.axis_size(axis)
        forward = [(i, i + 1) for i in range(count - 1)]
        backward = [(target, source) for source, target in forward]
        low = lax.ppermute(
            lax.slice_in_dim(block, block.shape[dim] - width, None, axis=dim), axis, forward
        )
        high = lax.ppermute(lax.slice_in_dim(block, 0, width, axis=dim), axis, backward)
        block = jnp.concatenate([low, block, high], axis=dim)
    return block


def box_coords(box_pos):
    box_count = box_pos.shape[0]
    slab_coord = (jnp.arange(box_count, dtype=jnp.int32) // (CY * CZ)).astype(jnp.float32)
    row_coord = (box_pos // CZ).astype(jnp.float32)
    col_coord = (box_pos % CZ).astype(jnp.float32)
    return (slab_coord, row_coord, col_coord)


def translator(column, coords):
    slab_gap = coords[0][:, None] - coords[0][None, :]
    row_gap = coords[1][:, None] - coords[1][None, :]
    col_gap = coords[2][:, None] - coords[2][None, :]
    square = slab_gap * slab_gap + row_gap * row_gap + col_gap * col_gap
    nearby = jnp.maximum(jnp.maximum(jnp.abs(slab_gap), jnp.abs(row_gap)), jnp.abs(col_gap)) < 1.5
    radius = jnp.sqrt(jnp.maximum(square, 1.0))
    kappa = wave_number * BSIDE
    argument = kappa * radius
    inverse = 1.0 / argument
    cosine = (column[0] * slab_gap + column[1] * row_gap + column[2] * col_gap) / radius
    prev_re, prev_im = (inverse, jnp.zeros_like(inverse))
    now_re, now_im = (jnp.zeros_like(inverse), -inverse)
    leg_prev, leg_now = (jnp.ones_like(inverse), jnp.ones_like(inverse))
    total_re = jnp.zeros_like(inverse)
    total_im = jnp.zeros_like(inverse)
    for order in range(4):
        if order == 0:
            legendre = jnp.ones_like(inverse)
        elif order == 1:
            legendre = cosine
        else:
            legendre = ((2 * order - 1) * cosine * leg_now - (order - 1) * leg_prev) / order
        leg_prev, leg_now = (leg_now, legendre)
        weight = (2.0 * order + 1.0) * legendre
        rot = order % 4
        if rot == 0:
            term_re, term_im = (now_re, now_im)
        elif rot == 1:
            term_re, term_im = (-now_im, now_re)
        elif rot == 2:
            term_re, term_im = (-now_re, -now_im)
        else:
            term_re, term_im = (now_im, -now_re)
        total_re = total_re + weight * term_re
        total_im = total_im + weight * term_im
        next_re = (2.0 * order + 1.0) * inverse * now_re - prev_re
        next_im = (2.0 * order + 1.0) * inverse * now_im - prev_im
        prev_re, prev_im = (now_re, now_im)
        now_re, now_im = (next_re, next_im)
    wave_re = jnp.cos(argument)
    wave_im = jnp.sin(argument)
    factor = jnp.where(nearby, 0.0, far_scale * kappa / 16.0)
    real_part = factor * (total_re * wave_re - total_im * wave_im)
    imag_part = factor * (total_re * wave_im + total_im * wave_re)
    return jnp.stack([real_part, imag_part]).astype(jnp.bfloat16)


def build_translators(dir_block, box_pos):
    coords = box_coords(box_pos)

    def one_direction(column):
        return translator(column, coords)

    return jax.vmap(one_direction)(jnp.transpose(dir_block))


def green_constants():
    index = np.arange(V)
    coords = np.stack([index // (BSIDE * BSIDE), index // BSIDE % BSIDE, index % BSIDE])
    blocks = []
    for base in range(8):
        offset = (base // 4, base // 2 % 2, base % 2)
        square = np.zeros((V, V), np.float64)
        for dimension in range(3):
            differ = coords[dimension][:, None] - coords[dimension][None, :] - BSIDE * offset[dimension]
            square = square + differ * differ
        radius = np.sqrt(np.maximum(square, 1.0))
        inside = square < 0.5
        real_part = np.where(inside, self_value, near_scale * np.cos(wave_number * radius) / radius)
        imag_part = np.where(inside, 0.0, near_scale * np.sin(wave_number * radius) / radius)
        blocks.append(np.concatenate([real_part, imag_part], axis=0))
    return np.stack(blocks).astype(np.float32)


def pair_tables():
    slab_of, pos_of, valid, flips = [], [], [], []
    for base in range(8):
        bx, by, bz = base // 4, base // 2 % 2, base % 2
        for target in range(CY * CZ):
            ty, tz = target // CZ, target % CZ
            for side in range(2):
                shift_x = 0 if bx == 0 else (1 if side == 0 else -1)
                slab_of.append(1 + shift_x)
                pos_of.append((ty ^ by) * CZ + (tz ^ bz))
                valid.append(1.0 if (bx == 1 or side == 0) else 0.0)
                flips.append((shift_x < 0, by == 1 and ty == 1, bz == 1 and tz == 1))
    return (np.array(slab_of), np.array(pos_of), np.array(valid, np.float32), np.array(flips))


def masked_flips(values, flips):
    cube = values.reshape(values.shape[:-1] + (BSIDE, BSIDE, BSIDE))
    lead = values.ndim - 1
    for dimension in range(3):
        mask = flips[:, dimension].reshape((-1,) + (1,) * (cube.ndim - 1))
        cube = jnp.where(mask, jnp.flip(cube, lead + dimension), cube)
    return cube.reshape(values.shape)


def near_field(sources, box_pos):
    exc_dev = sources.shape[1]
    box_dev = sources.shape[2]
    extended = padded(sources, (("box", 2),), box_dev)
    zeros_pos = jnp.zeros((box_dev,), jnp.int32)
    padded_pos = jnp.concatenate([zeros_pos, box_pos, zeros_pos])
    local_pos = lax.dynamic_slice_in_dim(padded_pos, lax.axis_index("box") * box_dev, 3 * box_dev)
    slab_of, pos_of, valid, flips = pair_tables()
    column_slab = np.arange(3 * box_dev) // box_dev
    selector = (
        (slab_of[:, None] == column_slab[None, :])
        & (pos_of[:, None] == local_pos[None, :])
    ).astype(jnp.float32) * valid[:, None]
    pieces = jnp.einsum(
        "pj,xejv->pxev", selector.astype(jnp.bfloat16), extended, preferred_element_type=jnp.float32
    ).astype(jnp.bfloat16)
    pieces = masked_flips(pieces, flips)
    pair_count = pieces.shape[0]
    rows = pieces.reshape(8, -1, V)
    blocks = jnp.asarray(green_constants(), jnp.bfloat16)
    product = lax.dot_general(
        rows, blocks, (((2,), (2,)), ((0,), (0,))), preferred_element_type=jnp.float32
    )
    product = product.reshape(pair_count, 2, exc_dev, 2, V)
    result = jnp.stack(
        [
            product[:, 0, :, 0] - product[:, 1, :, 1],
            product[:, 0, :, 1] + product[:, 1, :, 0],
        ],
        axis=1,
    )
    result = masked_flips(result, flips)
    per_slot = jnp.sum(result.reshape(8, CY * CZ, 2, 2, exc_dev, V), axis=(0, 2))
    own_pos = local_pos[box_dev : 2 * box_dev]
    choose = (own_pos[:, None] == jnp.arange(CY * CZ, dtype=jnp.int32)[None, :]).astype(jnp.float32)
    return jnp.sum(
        choose[None, None, :, :, None] * jnp.transpose(per_slot, (1, 2, 0, 3))[:, :, None], axis=3
    )


def encode(sources, enc_table):
    real_prod = jnp.einsum(
        "kv,xebv->kxeb", enc_table[0], sources, preferred_element_type=jnp.float32
    )
    imag_prod = jnp.einsum(
        "kv,xebv->kxeb", enc_table[1], sources, preferred_element_type=jnp.float32
    )
    return jnp.stack(
        [real_prod[:, 0] - imag_prod[:, 1], imag_prod[:, 0] + real_prod[:, 1]], axis=1
    ).astype(jnp.bfloat16)


def translate(encoded, translators):
    real_prod = jnp.einsum(
        "kts,kxes->kxet", translators[:, 0], encoded, preferred_element_type=jnp.float32
    )
    imag_prod = jnp.einsum(
        "kts,kxes->kxet", translators[:, 1], encoded, preferred_element_type=jnp.float32
    )
    return jnp.stack(
        [real_prod[:, 0] - imag_prod[:, 1], imag_prod[:, 0] + real_prod[:, 1]], axis=1
    ).astype(jnp.bfloat16)


def decode(returned, dec_table):
    real_prod = jnp.einsum(
        "vk,kxeb->xebv", dec_table[0], returned, preferred_element_type=jnp.float32
    )
    imag_prod = jnp.einsum(
        "vk,kxeb->xebv", dec_table[1], returned, preferred_element_type=jnp.float32
    )
    return jnp.stack([real_prod[0] - imag_prod[1], imag_prod[0] + real_prod[1]])


def shards(incident, contrast, box_pos, directions, enc_table, dec_table):
    contrast_real = contrast.astype(jnp.float32) * chi_step
    translators = build_translators(directions, box_pos)
    fields = incident
    outputs = []
    for term_index in range(2):
        sources = (contrast_real[None, None] * fields.astype(jnp.float32)).astype(jnp.bfloat16)
        near_part = near_field(sources, box_pos)
        encoded = encode(sources, enc_table)
        returned = lax.all_to_all(
            translate(
                lax.all_to_all(encoded, "box", split_axis=0, concat_axis=3, tiled=True), translators
            ),
            "box",
            split_axis=3,
            concat_axis=0,
            tiled=True,
        )
        fields = (near_part + decode(returned, dec_table)).astype(jnp.bfloat16)
        outputs.append(fields)
    first_sq = jnp.sum(jnp.square(outputs[0].astype(jnp.float32)), axis=(0, 1, 3))
    second_sq = jnp.sum(jnp.square(outputs[1].astype(jnp.float32)), axis=(0, 1, 3))
    first_sum, second_sum = lax.psum((first_sq, second_sq), "exc")
    entry_count = 2 * outputs[0].shape[1] * lax.axis_size("exc") * outputs[0].shape[3]
    series_ratio = jnp.sqrt(second_sum / entry_count / (first_sum / entry_count + epsilon))
    return (outputs[0], outputs[1], series_ratio)


def solution(mesh):
    placed = (P(None, "exc", "box", None), P("box", None), P(), P(None, "box"), P(), P())
    return jax.shard_map(
        shards,
        mesh=mesh,
        in_specs=placed,
        out_specs=(P(None, "exc", "box", None), P(None, "exc", "box", None), P("box")),
        check_vma=False,
    )
```

```python
import numpy as np
import jax
import jax.numpy as jnp
from jax import lax
from jax.sharding import PartitionSpec as P

BSIDE = 8
CY = 2
CZ = 2
V = 512


wave_number = 0.8
near_scale = 0.1
self_value = 1.0
far_scale = 0.25
chi_step = 0.0625
epsilon = 1e-06


def padded(block, sides, width):
    for axis, dim in sides:
        count = lax.axis_size(axis)
        forward = [(i, i + 1) for i in range(count - 1)]
        backward = [(target, source) for source, target in forward]
        low = lax.ppermute(
            lax.slice_in_dim(block, block.shape[dim] - width, None, axis=dim), axis, forward
        )
        high = lax.ppermute(lax.slice_in_dim(block, 0, width, axis=dim), axis, backward)
        block = jnp.concatenate([low, block, high], axis=dim)
    return block


def box_coords(box_pos):
    box_count = box_pos.shape[0]
    slab_coord = (jnp.arange(box_count, dtype=jnp.int32) // (CY * CZ)).astype(jnp.float32)
    row_coord = (box_pos // CZ).astype(jnp.float32)
    col_coord = (box_pos % CZ).astype(jnp.float32)
    return (slab_coord, row_coord, col_coord)


def translator(column, coords):
    slab_gap = coords[0][:, None] - coords[0][None, :]
    row_gap = coords[1][:, None] - coords[1][None, :]
    col_gap = coords[2][:, None] - coords[2][None, :]
    square = slab_gap * slab_gap + row_gap * row_gap + col_gap * col_gap
    nearby = jnp.maximum(jnp.maximum(jnp.abs(slab_gap), jnp.abs(row_gap)), jnp.abs(col_gap)) < 1.5
    radius = jnp.sqrt(jnp.maximum(square, 1.0))
    kappa = wave_number * BSIDE
    argument = kappa * radius
    inverse = 1.0 / argument
    cosine = (column[0] * slab_gap + column[1] * row_gap + column[2] * col_gap) / radius
    prev_re, prev_im = (inverse, jnp.zeros_like(inverse))
    now_re, now_im = (jnp.zeros_like(inverse), -inverse)
    leg_prev, leg_now = (jnp.ones_like(inverse), jnp.ones_like(inverse))
    total_re = jnp.zeros_like(inverse)
    total_im = jnp.zeros_like(inverse)
    for order in range(4):
        if order == 0:
            legendre = jnp.ones_like(inverse)
        elif order == 1:
            legendre = cosine
        else:
            legendre = ((2 * order - 1) * cosine * leg_now - (order - 1) * leg_prev) / order
        leg_prev, leg_now = (leg_now, legendre)
        weight = (2.0 * order + 1.0) * legendre
        rot = order % 4
        if rot == 0:
            term_re, term_im = (now_re, now_im)
        elif rot == 1:
            term_re, term_im = (-now_im, now_re)
        elif rot == 2:
            term_re, term_im = (-now_re, -now_im)
        else:
            term_re, term_im = (now_im, -now_re)
        total_re = total_re + weight * term_re
        total_im = total_im + weight * term_im
        next_re = (2.0 * order + 1.0) * inverse * now_re - prev_re
        next_im = (2.0 * order + 1.0) * inverse * now_im - prev_im
        prev_re, prev_im = (now_re, now_im)
        now_re, now_im = (next_re, next_im)
    wave_re = jnp.cos(argument)
    wave_im = jnp.sin(argument)
    factor = jnp.where(nearby, 0.0, far_scale * kappa / 16.0)
    real_part = factor * (total_re * wave_re - total_im * wave_im)
    imag_part = factor * (total_re * wave_im + total_im * wave_re)
    return jnp.stack([real_part, imag_part]).astype(jnp.bfloat16)


def build_translators(dir_block, box_pos):
    coords = box_coords(box_pos)

    def one_direction(column):
        return translator(column, coords)

    return jax.vmap(one_direction)(jnp.transpose(dir_block))


def green_constants():
    index = np.arange(V)
    coords = np.stack([index // (BSIDE * BSIDE), index // BSIDE % BSIDE, index % BSIDE])
    blocks = []
    for base in range(8):
        offset = (base // 4, base // 2 % 2, base % 2)
        square = np.zeros((V, V), np.float64)
        for dimension in range(3):
            differ = coords[dimension][:, None] - coords[dimension][None, :] - BSIDE * offset[dimension]
            square = square + differ * differ
        radius = np.sqrt(np.maximum(square, 1.0))
        inside = square < 0.5
        real_part = np.where(inside, self_value, near_scale * np.cos(wave_number * radius) / radius)
        imag_part = np.where(inside, 0.0, near_scale * np.sin(wave_number * radius) / radius)
        blocks.append(np.concatenate([real_part, imag_part], axis=0))
    return np.stack(blocks).astype(np.float32)


def pair_tables():
    slab_of, pos_of, valid, flips = [], [], [], []
    for base in range(8):
        bx, by, bz = base // 4, base // 2 % 2, base % 2
        for target in range(CY * CZ):
            ty, tz = target // CZ, target % CZ
            for side in range(2):
                shift_x = 0 if bx == 0 else (1 if side == 0 else -1)
                slab_of.append(1 + shift_x)
                pos_of.append((ty ^ by) * CZ + (tz ^ bz))
                valid.append(1.0 if (bx == 1 or side == 0) else 0.0)
                flips.append((shift_x < 0, by == 1 and ty == 1, bz == 1 and tz == 1))
    return (np.array(slab_of), np.array(pos_of), np.array(valid, np.float32), np.array(flips))


def flip_matrices():
    index = np.arange(V)
    coords = [index // (BSIDE * BSIDE), index // BSIDE % BSIDE, index % BSIDE]
    matrices = []
    for dimension in range(3):
        moved = list(coords)
        moved[dimension] = BSIDE - 1 - coords[dimension]
        source = moved[0] * BSIDE * BSIDE + moved[1] * BSIDE + moved[2]
        matrices.append((source[None, :] == index[:, None]).astype(np.float32))
    return matrices


def masked_flips(rows, masks, precision):
    for matrix, mask in zip(flip_matrices(), masks):
        flipped = jnp.dot(
            rows, jnp.asarray(matrix, rows.dtype), precision=precision,
            preferred_element_type=jnp.float32,
        ).astype(rows.dtype)
        rows = jnp.where(mask[:, None], flipped, rows)
    return rows


def near_field(sources, box_pos):
    exc_dev = sources.shape[1]
    box_dev = sources.shape[2]
    slots = CY * CZ
    extended = padded(sources, (("box", 2),), box_dev)
    zeros_pos = jnp.zeros((box_dev,), jnp.int32)
    padded_pos = jnp.concatenate([zeros_pos, box_pos, zeros_pos])
    local_pos = lax.dynamic_slice_in_dim(padded_pos, lax.axis_index("box") * box_dev, 3 * box_dev)
    slab_of, pos_of, valid, flips = pair_tables()
    column_slab = np.arange(3 * box_dev) // box_dev
    selector = (
        (slab_of[:, None] == column_slab[None, :])
        & (pos_of[:, None] == local_pos[None, :])
    ).astype(jnp.float32) * valid[:, None]
    selector = selector.reshape(8, 1, slots, 2, 1, 1, 1, 3 * box_dev)
    part_eye = np.eye(2, dtype=np.float32).reshape(1, 2, 1, 1, 1, 2, 1, 1)
    exc_eye = np.eye(exc_dev, dtype=np.float32).reshape(1, 1, 1, 1, exc_dev, 1, exc_dev, 1)
    gather = (selector * part_eye * exc_eye).reshape(-1, 2 * exc_dev * 3 * box_dev)
    pieces = jnp.dot(
        gather.astype(jnp.bfloat16), extended.reshape(-1, V), preferred_element_type=jnp.float32
    ).astype(jnp.bfloat16)
    row_flips = np.broadcast_to(
        flips.reshape(8, 1, slots, 2, 1, 3), (8, 2, slots, 2, exc_dev, 3)
    ).reshape(-1, 3)
    masks = [row_flips[:, d] for d in range(3)]
    pieces = masked_flips(pieces, masks, None)
    blocks = jnp.asarray(green_constants(), jnp.bfloat16)
    product = lax.dot_general(
        pieces.reshape(8, -1, V), blocks, (((2,), (2,)), ((0,), (0,))),
        preferred_element_type=jnp.float32,
    )
    product = product.reshape(8, 2, -1, 2, V)
    result = jnp.stack(
        [
            product[:, 0, :, 0] - product[:, 1, :, 1],
            product[:, 0, :, 1] + product[:, 1, :, 0],
        ],
        axis=1,
    ).reshape(-1, V)
    result = masked_flips(result, masks, lax.Precision.HIGHEST)
    own_pos = local_pos[box_dev : 2 * box_dev]
    choose = (own_pos[:, None] == jnp.arange(slots, dtype=jnp.int32)[None, :]).astype(jnp.float32)
    choose = choose.reshape(1, 1, box_dev, 1, 1, slots, 1, 1)
    part_eye = np.eye(2, dtype=np.float32).reshape(2, 1, 1, 1, 2, 1, 1, 1)
    exc_eye = np.eye(exc_dev, dtype=np.float32).reshape(1, exc_dev, 1, 1, 1, 1, 1, exc_dev)
    ones = np.ones((1, 1, 1, 8, 1, 1, 2, 1), np.float32)
    summing = (choose * part_eye * exc_eye * ones).reshape(2 * exc_dev * box_dev, -1)
    placed = jnp.dot(summing, result, precision=lax.Precision.HIGHEST)
    return placed.reshape(2, exc_dev, box_dev, V)


def encode(sources, enc_table):
    real_prod = jnp.einsum(
        "kv,xebv->kxeb", enc_table[0], sources, preferred_element_type=jnp.float32
    )
    imag_prod = jnp.einsum(
        "kv,xebv->kxeb", enc_table[1], sources, preferred_element_type=jnp.float32
    )
    return jnp.stack(
        [real_prod[:, 0] - imag_prod[:, 1], imag_prod[:, 0] + real_prod[:, 1]], axis=1
    ).astype(jnp.bfloat16)


def translate(encoded, translators):
    real_prod = jnp.einsum(
        "kts,kxes->kxet", translators[:, 0], encoded, preferred_element_type=jnp.float32
    )
    imag_prod = jnp.einsum(
        "kts,kxes->kxet", translators[:, 1], encoded, preferred_element_type=jnp.float32
    )
    return jnp.stack(
        [real_prod[:, 0] - imag_prod[:, 1], imag_prod[:, 0] + real_prod[:, 1]], axis=1
    ).astype(jnp.bfloat16)


def decode(returned, dec_table):
    real_prod = jnp.einsum(
        "vk,kxeb->xebv", dec_table[0], returned, preferred_element_type=jnp.float32
    )
    imag_prod = jnp.einsum(
        "vk,kxeb->xebv", dec_table[1], returned, preferred_element_type=jnp.float32
    )
    return jnp.stack([real_prod[0] - imag_prod[1], imag_prod[0] + real_prod[1]])


def shards(incident, contrast, box_pos, directions, enc_table, dec_table):
    contrast_real = contrast.astype(jnp.float32) * chi_step
    translators = build_translators(directions, box_pos)
    fields = incident
    outputs = []
    for term_index in range(2):
        sources = (contrast_real[None, None] * fields.astype(jnp.float32)).astype(jnp.bfloat16)
        near_part = near_field(sources, box_pos)
        encoded = encode(sources, enc_table)
        returned = lax.all_to_all(
            translate(
                lax.all_to_all(encoded, "box", split_axis=0, concat_axis=3, tiled=True), translators
            ),
            "box",
            split_axis=3,
            concat_axis=0,
            tiled=True,
        )
        fields = (near_part + decode(returned, dec_table)).astype(jnp.bfloat16)
        outputs.append(fields)
    first_sq = jnp.sum(jnp.square(outputs[0].astype(jnp.float32)), axis=(0, 1, 3))
    second_sq = jnp.sum(jnp.square(outputs[1].astype(jnp.float32)), axis=(0, 1, 3))
    first_sum, second_sum = lax.psum((first_sq, second_sq), "exc")
    entry_count = 2 * outputs[0].shape[1] * lax.axis_size("exc") * outputs[0].shape[3]
    series_ratio = jnp.sqrt(second_sum / entry_count / (first_sum / entry_count + epsilon))
    return (outputs[0], outputs[1], series_ratio)


def solution(mesh):
    placed = (P(None, "exc", "box", None), P("box", None), P(), P(None, "box"), P(), P())
    return jax.shard_map(
        shards,
        mesh=mesh,
        in_specs=placed,
        out_specs=(P(None, "exc", "box", None), P(None, "exc", "box", None), P("box")),
        check_vma=False,
    )
```

```python
import numpy as np
import jax
import jax.numpy as jnp
from jax import lax
from jax.sharding import PartitionSpec as P

BSIDE = 8
CY = 2
CZ = 2
V = 512


wave_number = 0.8
near_scale = 0.1
self_value = 1.0
far_scale = 0.25
chi_step = 0.0625
epsilon = 1e-06
BOX = ("x", "ylo", "z")


def padded(block, sides, width):
    for axis, dim in sides:
        count = lax.axis_size(axis)
        forward = [(i, i + 1) for i in range(count - 1)]
        backward = [(target, source) for source, target in forward]
        low = lax.ppermute(
            lax.slice_in_dim(block, block.shape[dim] - width, None, axis=dim), axis, forward
        )
        high = lax.ppermute(lax.slice_in_dim(block, 0, width, axis=dim), axis, backward)
        block = jnp.concatenate([low, block, high], axis=dim)
    return block


def spread_directions(encoded):
    plane = lax.axis_size(("x", "ylo"))
    line = lax.axis_size("z")
    per = encoded.shape[0] // (plane * line)
    parts = encoded.reshape((plane, line, per) + encoded.shape[1:])
    parts = lax.all_to_all(parts, "z", split_axis=1, concat_axis=1, tiled=True)
    parts = lax.all_to_all(parts, ("x", "ylo"), split_axis=0, concat_axis=0, tiled=True)
    parts = jnp.transpose(parts, (2, 3, 4, 0, 1, 5))
    return parts.reshape(parts.shape[:3] + (-1,))


def collect_boxes(translated):
    plane = lax.axis_size(("x", "ylo"))
    line = lax.axis_size("z")
    per = translated.shape[3] // (plane * line)
    parts = translated.reshape(translated.shape[:3] + (plane, line, per))
    parts = jnp.transpose(parts, (3, 4, 0, 1, 2, 5))
    parts = lax.all_to_all(parts, ("x", "ylo"), split_axis=0, concat_axis=0, tiled=True)
    parts = lax.all_to_all(parts, "z", split_axis=1, concat_axis=1, tiled=True)
    return parts.reshape((-1,) + parts.shape[3:])


def box_coords(box_pos):
    box_count = box_pos.shape[0]
    slab_coord = (jnp.arange(box_count, dtype=jnp.int32) // (CY * CZ)).astype(jnp.float32)
    row_coord = (box_pos // CZ).astype(jnp.float32)
    col_coord = (box_pos % CZ).astype(jnp.float32)
    return (slab_coord, row_coord, col_coord)


def translator(column, coords):
    slab_gap = coords[0][:, None] - coords[0][None, :]
    row_gap = coords[1][:, None] - coords[1][None, :]
    col_gap = coords[2][:, None] - coords[2][None, :]
    square = slab_gap * slab_gap + row_gap * row_gap + col_gap * col_gap
    nearby = jnp.maximum(jnp.maximum(jnp.abs(slab_gap), jnp.abs(row_gap)), jnp.abs(col_gap)) < 1.5
    radius = jnp.sqrt(jnp.maximum(square, 1.0))
    kappa = wave_number * BSIDE
    argument = kappa * radius
    inverse = 1.0 / argument
    cosine = (column[0] * slab_gap + column[1] * row_gap + column[2] * col_gap) / radius
    prev_re, prev_im = (inverse, jnp.zeros_like(inverse))
    now_re, now_im = (jnp.zeros_like(inverse), -inverse)
    leg_prev, leg_now = (jnp.ones_like(inverse), jnp.ones_like(inverse))
    total_re = jnp.zeros_like(inverse)
    total_im = jnp.zeros_like(inverse)
    for order in range(4):
        if order == 0:
            legendre = jnp.ones_like(inverse)
        elif order == 1:
            legendre = cosine
        else:
            legendre = ((2 * order - 1) * cosine * leg_now - (order - 1) * leg_prev) / order
        leg_prev, leg_now = (leg_now, legendre)
        weight = (2.0 * order + 1.0) * legendre
        rot = order % 4
        if rot == 0:
            term_re, term_im = (now_re, now_im)
        elif rot == 1:
            term_re, term_im = (-now_im, now_re)
        elif rot == 2:
            term_re, term_im = (-now_re, -now_im)
        else:
            term_re, term_im = (now_im, -now_re)
        total_re = total_re + weight * term_re
        total_im = total_im + weight * term_im
        next_re = (2.0 * order + 1.0) * inverse * now_re - prev_re
        next_im = (2.0 * order + 1.0) * inverse * now_im - prev_im
        prev_re, prev_im = (now_re, now_im)
        now_re, now_im = (next_re, next_im)
    wave_re = jnp.cos(argument)
    wave_im = jnp.sin(argument)
    factor = jnp.where(nearby, 0.0, far_scale * kappa / 16.0)
    real_part = factor * (total_re * wave_re - total_im * wave_im)
    imag_part = factor * (total_re * wave_im + total_im * wave_re)
    return jnp.stack([real_part, imag_part]).astype(jnp.bfloat16)


def build_translators(dir_block, box_pos):
    coords = box_coords(box_pos)

    def one_direction(column):
        return translator(column, coords)

    return jax.vmap(one_direction)(jnp.transpose(dir_block))


def green_constants():
    index = np.arange(V)
    coords = np.stack([index // (BSIDE * BSIDE), index // BSIDE % BSIDE, index % BSIDE])
    blocks = []
    for base in range(8):
        offset = (base // 4, base // 2 % 2, base % 2)
        square = np.zeros((V, V), np.float64)
        for dimension in range(3):
            differ = coords[dimension][:, None] - coords[dimension][None, :] - BSIDE * offset[dimension]
            square = square + differ * differ
        radius = np.sqrt(np.maximum(square, 1.0))
        inside = square < 0.5
        real_part = np.where(inside, self_value, near_scale * np.cos(wave_number * radius) / radius)
        imag_part = np.where(inside, 0.0, near_scale * np.sin(wave_number * radius) / radius)
        blocks.append(np.concatenate([real_part, imag_part], axis=0))
    return np.stack(blocks).astype(np.float32)


def pair_tables():
    slab_of, pos_of, valid, flips = [], [], [], []
    for base in range(8):
        bx, by, bz = base // 4, base // 2 % 2, base % 2
        for target in range(CY * CZ):
            ty, tz = target // CZ, target % CZ
            for side in range(2):
                shift_x = 0 if bx == 0 else (1 if side == 0 else -1)
                slab_of.append(1 + shift_x)
                pos_of.append((ty ^ by) * CZ + (tz ^ bz))
                valid.append(1.0 if (bx == 1 or side == 0) else 0.0)
                flips.append((shift_x < 0, by == 1 and ty == 1, bz == 1 and tz == 1))
    return (np.array(slab_of), np.array(pos_of), np.array(valid, np.float32), np.array(flips))


def flip_matrices():
    index = np.arange(V)
    coords = [index // (BSIDE * BSIDE), index // BSIDE % BSIDE, index % BSIDE]
    matrices = []
    for dimension in range(3):
        moved = list(coords)
        moved[dimension] = BSIDE - 1 - coords[dimension]
        source = moved[0] * BSIDE * BSIDE + moved[1] * BSIDE + moved[2]
        matrices.append((source[None, :] == index[:, None]).astype(np.float32))
    return matrices


def masked_flips(rows, masks, precision):
    for matrix, mask in zip(flip_matrices(), masks):
        flipped = jnp.dot(
            rows, jnp.asarray(matrix, rows.dtype), precision=precision,
            preferred_element_type=jnp.float32,
        ).astype(rows.dtype)
        rows = jnp.where(mask[:, None], flipped, rows)
    return rows


def near_field(sources, box_pos):
    exc_dev = sources.shape[1]
    box_dev = sources.shape[2]
    slots = CY * CZ
    extended = padded(sources, ((BOX, 2),), box_dev)
    zeros_pos = jnp.zeros((box_dev,), jnp.int32)
    padded_pos = jnp.concatenate([zeros_pos, box_pos, zeros_pos])
    local_pos = lax.dynamic_slice_in_dim(padded_pos, lax.axis_index(BOX) * box_dev, 3 * box_dev)
    slab_of, pos_of, valid, flips = pair_tables()
    column_slab = np.arange(3 * box_dev) // box_dev
    selector = (
        (slab_of[:, None] == column_slab[None, :])
        & (pos_of[:, None] == local_pos[None, :])
    ).astype(jnp.float32) * valid[:, None]
    selector = selector.reshape(8, 1, slots, 2, 1, 1, 1, 3 * box_dev)
    part_eye = np.eye(2, dtype=np.float32).reshape(1, 2, 1, 1, 1, 2, 1, 1)
    exc_eye = np.eye(exc_dev, dtype=np.float32).reshape(1, 1, 1, 1, exc_dev, 1, exc_dev, 1)
    gather = (selector * part_eye * exc_eye).reshape(-1, 2 * exc_dev * 3 * box_dev)
    pieces = jnp.dot(
        gather.astype(jnp.bfloat16), extended.reshape(-1, V), preferred_element_type=jnp.float32
    ).astype(jnp.bfloat16)
    row_flips = np.broadcast_to(
        flips.reshape(8, 1, slots, 2, 1, 3), (8, 2, slots, 2, exc_dev, 3)
    ).reshape(-1, 3)
    masks = [row_flips[:, d] for d in range(3)]
    pieces = masked_flips(pieces, masks, None)
    blocks = jnp.asarray(green_constants(), jnp.bfloat16)
    product = lax.dot_general(
        pieces.reshape(8, -1, V), blocks, (((2,), (2,)), ((0,), (0,))),
        preferred_element_type=jnp.float32,
    )
    product = product.reshape(8, 2, -1, 2, V)
    result = jnp.stack(
        [
            product[:, 0, :, 0] - product[:, 1, :, 1],
            product[:, 0, :, 1] + product[:, 1, :, 0],
        ],
        axis=1,
    ).reshape(-1, V)
    result = masked_flips(result, masks, lax.Precision.HIGHEST)
    own_pos = local_pos[box_dev : 2 * box_dev]
    choose = (own_pos[:, None] == jnp.arange(slots, dtype=jnp.int32)[None, :]).astype(jnp.float32)
    choose = choose.reshape(1, 1, box_dev, 1, 1, slots, 1, 1)
    part_eye = np.eye(2, dtype=np.float32).reshape(2, 1, 1, 1, 2, 1, 1, 1)
    exc_eye = np.eye(exc_dev, dtype=np.float32).reshape(1, exc_dev, 1, 1, 1, 1, 1, exc_dev)
    ones = np.ones((1, 1, 1, 8, 1, 1, 2, 1), np.float32)
    summing = (choose * part_eye * exc_eye * ones).reshape(2 * exc_dev * box_dev, -1)
    placed = jnp.dot(summing, result, precision=lax.Precision.HIGHEST)
    return placed.reshape(2, exc_dev, box_dev, V)


def encode(sources, enc_table):
    real_prod = jnp.einsum(
        "kv,xebv->kxeb", enc_table[0], sources, preferred_element_type=jnp.float32
    )
    imag_prod = jnp.einsum(
        "kv,xebv->kxeb", enc_table[1], sources, preferred_element_type=jnp.float32
    )
    return jnp.stack(
        [real_prod[:, 0] - imag_prod[:, 1], imag_prod[:, 0] + real_prod[:, 1]], axis=1
    ).astype(jnp.bfloat16)


def translate(encoded, translators):
    real_prod = jnp.einsum(
        "kts,kxes->kxet", translators[:, 0], encoded, preferred_element_type=jnp.float32
    )
    imag_prod = jnp.einsum(
        "kts,kxes->kxet", translators[:, 1], encoded, preferred_element_type=jnp.float32
    )
    return jnp.stack(
        [real_prod[:, 0] - imag_prod[:, 1], imag_prod[:, 0] + real_prod[:, 1]], axis=1
    ).astype(jnp.bfloat16)


def decode(returned, dec_table):
    real_prod = jnp.einsum(
        "vk,kxeb->xebv", dec_table[0], returned, preferred_element_type=jnp.float32
    )
    imag_prod = jnp.einsum(
        "vk,kxeb->xebv", dec_table[1], returned, preferred_element_type=jnp.float32
    )
    return jnp.stack([real_prod[0] - imag_prod[1], imag_prod[0] + real_prod[1]])


def shards(incident, contrast, box_pos, directions, enc_table, dec_table):
    contrast_real = contrast.astype(jnp.float32) * chi_step
    translators = build_translators(directions, box_pos)
    fields = incident
    outputs = []
    for term_index in range(2):
        sources = (contrast_real[None, None] * fields.astype(jnp.float32)).astype(jnp.bfloat16)
        near_part = near_field(sources, box_pos)
        encoded = encode(sources, enc_table)
        returned = collect_boxes(translate(spread_directions(encoded), translators))
        fields = (near_part + decode(returned, dec_table)).astype(jnp.bfloat16)
        outputs.append(fields)
    first_sq = jnp.sum(jnp.square(outputs[0].astype(jnp.float32)), axis=(0, 1, 3))
    second_sq = jnp.sum(jnp.square(outputs[1].astype(jnp.float32)), axis=(0, 1, 3))
    first_sum, second_sum = lax.psum((first_sq, second_sq), "exc")
    entry_count = 2 * outputs[0].shape[1] * lax.axis_size("exc") * outputs[0].shape[3]
    series_ratio = jnp.sqrt(second_sum / entry_count / (first_sum / entry_count + epsilon))
    return (outputs[0], outputs[1], series_ratio)


def solution(mesh):
    fine = jax.sharding.Mesh(mesh.devices.reshape(4, 4, 8, mesh.shape["exc"]), BOX + ("exc",))
    placed = (P(None, "exc", BOX, None), P(BOX, None), P(), P(None, BOX), P(), P())
    return jax.shard_map(
        shards,
        mesh=fine,
        in_specs=placed,
        out_specs=(P(None, "exc", BOX, None), P(None, "exc", BOX, None), P(BOX)),
        check_vma=False,
    )
```

```python
import numpy as np
import jax
import jax.numpy as jnp
from jax import lax
from jax.sharding import PartitionSpec as P

BSIDE = 8
CY = 2
CZ = 2
V = 512


wave_number = 0.8
near_scale = 0.1
self_value = 1.0
far_scale = 0.25
chi_step = 0.0625
epsilon = 1e-06
BOX = ("x", "ylo", "z")


def padded(block, sides, width):
    for axis, dim in sides:
        count = lax.axis_size(axis)
        forward = [(i, i + 1) for i in range(count - 1)]
        backward = [(target, source) for source, target in forward]
        low = lax.ppermute(
            lax.slice_in_dim(block, block.shape[dim] - width, None, axis=dim), axis, forward
        )
        high = lax.ppermute(lax.slice_in_dim(block, 0, width, axis=dim), axis, backward)
        block = jnp.concatenate([low, block, high], axis=dim)
    return block


def spread_directions(encoded):
    return lax.all_to_all(encoded, BOX, split_axis=0, concat_axis=3, tiled=True)


def collect_boxes(translated):
    plane = lax.axis_size(("x", "ylo"))
    line = lax.axis_size("z")
    per = translated.shape[3] // (plane * line)
    parts = translated.reshape(translated.shape[:3] + (plane, line, per))
    parts = jnp.transpose(parts, (3, 4, 0, 1, 2, 5))
    parts = lax.all_to_all(parts, ("x", "ylo"), split_axis=0, concat_axis=0, tiled=True)
    parts = lax.all_to_all(parts, "z", split_axis=1, concat_axis=1, tiled=True)
    return parts.reshape((-1,) + parts.shape[3:])


def box_coords(box_pos):
    box_count = box_pos.shape[0]
    slab_coord = (jnp.arange(box_count, dtype=jnp.int32) // (CY * CZ)).astype(jnp.float32)
    row_coord = (box_pos // CZ).astype(jnp.float32)
    col_coord = (box_pos % CZ).astype(jnp.float32)
    return (slab_coord, row_coord, col_coord)


def translator(column, coords):
    slab_gap = coords[0][:, None] - coords[0][None, :]
    row_gap = coords[1][:, None] - coords[1][None, :]
    col_gap = coords[2][:, None] - coords[2][None, :]
    square = slab_gap * slab_gap + row_gap * row_gap + col_gap * col_gap
    nearby = jnp.maximum(jnp.maximum(jnp.abs(slab_gap), jnp.abs(row_gap)), jnp.abs(col_gap)) < 1.5
    radius = jnp.sqrt(jnp.maximum(square, 1.0))
    kappa = wave_number * BSIDE
    argument = kappa * radius
    inverse = 1.0 / argument
    cosine = (column[0] * slab_gap + column[1] * row_gap + column[2] * col_gap) / radius
    prev_re, prev_im = (inverse, jnp.zeros_like(inverse))
    now_re, now_im = (jnp.zeros_like(inverse), -inverse)
    leg_prev, leg_now = (jnp.ones_like(inverse), jnp.ones_like(inverse))
    total_re = jnp.zeros_like(inverse)
    total_im = jnp.zeros_like(inverse)
    for order in range(4):
        if order == 0:
            legendre = jnp.ones_like(inverse)
        elif order == 1:
            legendre = cosine
        else:
            legendre = ((2 * order - 1) * cosine * leg_now - (order - 1) * leg_prev) / order
        leg_prev, leg_now = (leg_now, legendre)
        weight = (2.0 * order + 1.0) * legendre
        rot = order % 4
        if rot == 0:
            term_re, term_im = (now_re, now_im)
        elif rot == 1:
            term_re, term_im = (-now_im, now_re)
        elif rot == 2:
            term_re, term_im = (-now_re, -now_im)
        else:
            term_re, term_im = (now_im, -now_re)
        total_re = total_re + weight * term_re
        total_im = total_im + weight * term_im
        next_re = (2.0 * order + 1.0) * inverse * now_re - prev_re
        next_im = (2.0 * order + 1.0) * inverse * now_im - prev_im
        prev_re, prev_im = (now_re, now_im)
        now_re, now_im = (next_re, next_im)
    wave_re = jnp.cos(argument)
    wave_im = jnp.sin(argument)
    factor = jnp.where(nearby, 0.0, far_scale * kappa / 16.0)
    real_part = factor * (total_re * wave_re - total_im * wave_im)
    imag_part = factor * (total_re * wave_im + total_im * wave_re)
    return jnp.stack([real_part, imag_part]).astype(jnp.bfloat16)


def build_translators(dir_block, box_pos):
    coords = box_coords(box_pos)

    def one_direction(column):
        return translator(column, coords)

    return jax.vmap(one_direction)(jnp.transpose(dir_block))


def green_constants():
    index = np.arange(V)
    coords = np.stack([index // (BSIDE * BSIDE), index // BSIDE % BSIDE, index % BSIDE])
    blocks = []
    for base in range(8):
        offset = (base // 4, base // 2 % 2, base % 2)
        square = np.zeros((V, V), np.float64)
        for dimension in range(3):
            differ = coords[dimension][:, None] - coords[dimension][None, :] - BSIDE * offset[dimension]
            square = square + differ * differ
        radius = np.sqrt(np.maximum(square, 1.0))
        inside = square < 0.5
        real_part = np.where(inside, self_value, near_scale * np.cos(wave_number * radius) / radius)
        imag_part = np.where(inside, 0.0, near_scale * np.sin(wave_number * radius) / radius)
        blocks.append(np.concatenate([real_part, imag_part], axis=0))
    return np.stack(blocks).astype(np.float32)


def pair_tables():
    slab_of, pos_of, valid, flips = [], [], [], []
    for base in range(8):
        bx, by, bz = base // 4, base // 2 % 2, base % 2
        for target in range(CY * CZ):
            ty, tz = target // CZ, target % CZ
            for side in range(2):
                shift_x = 0 if bx == 0 else (1 if side == 0 else -1)
                slab_of.append(1 + shift_x)
                pos_of.append((ty ^ by) * CZ + (tz ^ bz))
                valid.append(1.0 if (bx == 1 or side == 0) else 0.0)
                flips.append((shift_x < 0, by == 1 and ty == 1, bz == 1 and tz == 1))
    return (np.array(slab_of), np.array(pos_of), np.array(valid, np.float32), np.array(flips))


def flip_matrices():
    index = np.arange(V)
    coords = [index // (BSIDE * BSIDE), index // BSIDE % BSIDE, index % BSIDE]
    matrices = []
    for dimension in range(3):
        moved = list(coords)
        moved[dimension] = BSIDE - 1 - coords[dimension]
        source = moved[0] * BSIDE * BSIDE + moved[1] * BSIDE + moved[2]
        matrices.append((source[None, :] == index[:, None]).astype(np.float32))
    return matrices


def masked_flips(rows, masks, precision):
    for matrix, mask in zip(flip_matrices(), masks):
        flipped = jnp.dot(
            rows, jnp.asarray(matrix, rows.dtype), precision=precision,
            preferred_element_type=jnp.float32,
        ).astype(rows.dtype)
        rows = jnp.where(mask[:, None], flipped, rows)
    return rows


def near_field(sources, box_pos):
    exc_dev = sources.shape[1]
    box_dev = sources.shape[2]
    slots = CY * CZ
    extended = padded(sources, ((BOX, 2),), box_dev)
    zeros_pos = jnp.zeros((box_dev,), jnp.int32)
    padded_pos = jnp.concatenate([zeros_pos, box_pos, zeros_pos])
    local_pos = lax.dynamic_slice_in_dim(padded_pos, lax.axis_index(BOX) * box_dev, 3 * box_dev)
    slab_of, pos_of, valid, flips = pair_tables()
    column_slab = np.arange(3 * box_dev) // box_dev
    selector = (
        (slab_of[:, None] == column_slab[None, :])
        & (pos_of[:, None] == local_pos[None, :])
    ).astype(jnp.float32) * valid[:, None]
    selector = selector.reshape(8, 1, slots, 2, 1, 1, 1, 3 * box_dev)
    part_eye = np.eye(2, dtype=np.float32).reshape(1, 2, 1, 1, 1, 2, 1, 1)
    exc_eye = np.eye(exc_dev, dtype=np.float32).reshape(1, 1, 1, 1, exc_dev, 1, exc_dev, 1)
    gather = (selector * part_eye * exc_eye).reshape(-1, 2 * exc_dev * 3 * box_dev)
    pieces = jnp.dot(
        gather.astype(jnp.bfloat16), extended.reshape(-1, V), preferred_element_type=jnp.float32
    ).astype(jnp.bfloat16)
    row_flips = np.broadcast_to(
        flips.reshape(8, 1, slots, 2, 1, 3), (8, 2, slots, 2, exc_dev, 3)
    ).reshape(-1, 3)
    masks = [row_flips[:, d] for d in range(3)]
    pieces = masked_flips(pieces, masks, None)
    blocks = jnp.asarray(green_constants(), jnp.bfloat16)
    product = lax.dot_general(
        pieces.reshape(8, -1, V), blocks, (((2,), (2,)), ((0,), (0,))),
        preferred_element_type=jnp.float32,
    )
    product = product.reshape(8, 2, -1, 2, V)
    result = jnp.stack(
        [
            product[:, 0, :, 0] - product[:, 1, :, 1],
            product[:, 0, :, 1] + product[:, 1, :, 0],
        ],
        axis=1,
    ).reshape(-1, V)
    result = masked_flips(result, masks, lax.Precision.HIGHEST)
    own_pos = local_pos[box_dev : 2 * box_dev]
    choose = (own_pos[:, None] == jnp.arange(slots, dtype=jnp.int32)[None, :]).astype(jnp.float32)
    choose = choose.reshape(1, 1, box_dev, 1, 1, slots, 1, 1)
    part_eye = np.eye(2, dtype=np.float32).reshape(2, 1, 1, 1, 2, 1, 1, 1)
    exc_eye = np.eye(exc_dev, dtype=np.float32).reshape(1, exc_dev, 1, 1, 1, 1, 1, exc_dev)
    ones = np.ones((1, 1, 1, 8, 1, 1, 2, 1), np.float32)
    summing = (choose * part_eye * exc_eye * ones).reshape(2 * exc_dev * box_dev, -1)
    placed = jnp.dot(summing, result, precision=lax.Precision.HIGHEST)
    return placed.reshape(2, exc_dev, box_dev, V)


def encode(sources, enc_table):
    real_prod = jnp.einsum(
        "kv,xebv->kxeb", enc_table[0], sources, preferred_element_type=jnp.float32
    )
    imag_prod = jnp.einsum(
        "kv,xebv->kxeb", enc_table[1], sources, preferred_element_type=jnp.float32
    )
    return jnp.stack(
        [real_prod[:, 0] - imag_prod[:, 1], imag_prod[:, 0] + real_prod[:, 1]], axis=1
    ).astype(jnp.bfloat16)


def translate(encoded, translators):
    real_prod = jnp.einsum(
        "kts,kxes->kxet", translators[:, 0], encoded, preferred_element_type=jnp.float32
    )
    imag_prod = jnp.einsum(
        "kts,kxes->kxet", translators[:, 1], encoded, preferred_element_type=jnp.float32
    )
    return jnp.stack(
        [real_prod[:, 0] - imag_prod[:, 1], imag_prod[:, 0] + real_prod[:, 1]], axis=1
    ).astype(jnp.bfloat16)


def decode(returned, dec_table):
    real_prod = jnp.einsum(
        "vk,kxeb->xebv", dec_table[0], returned, preferred_element_type=jnp.float32
    )
    imag_prod = jnp.einsum(
        "vk,kxeb->xebv", dec_table[1], returned, preferred_element_type=jnp.float32
    )
    return jnp.stack([real_prod[0] - imag_prod[1], imag_prod[0] + real_prod[1]])


def shards(incident, contrast, box_pos, directions, enc_table, dec_table):
    contrast_real = contrast.astype(jnp.float32) * chi_step
    translators = build_translators(directions, box_pos)
    fields = incident
    outputs = []
    for term_index in range(2):
        sources = (contrast_real[None, None] * fields.astype(jnp.float32)).astype(jnp.bfloat16)
        near_part = near_field(sources, box_pos)
        encoded = encode(sources, enc_table)
        returned = collect_boxes(translate(spread_directions(encoded), translators))
        fields = (near_part + decode(returned, dec_table)).astype(jnp.bfloat16)
        outputs.append(fields)
    first_sq = jnp.sum(jnp.square(outputs[0].astype(jnp.float32)), axis=(0, 1, 3))
    second_sq = jnp.sum(jnp.square(outputs[1].astype(jnp.float32)), axis=(0, 1, 3))
    stats = jnp.stack([first_sq, second_sq])
    peers = lax.axis_size("exc")
    spread = jnp.broadcast_to(stats[None], (peers,) + stats.shape)
    gathered = lax.all_to_all(spread, "exc", split_axis=0, concat_axis=0, tiled=True)
    first_sum, second_sum = jnp.sum(gathered, axis=0)
    entry_count = 2 * outputs[0].shape[1] * lax.axis_size("exc") * outputs[0].shape[3]
    series_ratio = jnp.sqrt(second_sum / entry_count / (first_sum / entry_count + epsilon))
    return (outputs[0], outputs[1], series_ratio)


def solution(mesh):
    fine = jax.sharding.Mesh(mesh.devices.reshape(4, 4, 8, mesh.shape["exc"]), BOX + ("exc",))
    placed = (P(None, "exc", BOX, None), P(BOX, None), P(), P(None, BOX), P(), P())
    return jax.shard_map(
        shards,
        mesh=fine,
        in_specs=placed,
        out_specs=(P(None, "exc", BOX, None), P(None, "exc", BOX, None), P(BOX)),
        check_vma=False,
    )
```

```python
import numpy as np
import jax
import jax.numpy as jnp
from jax import lax
from jax.sharding import PartitionSpec as P

BSIDE = 8
CY = 2
CZ = 2
V = 512


wave_number = 0.8
near_scale = 0.1
self_value = 1.0
far_scale = 0.25
chi_step = 0.0625
epsilon = 1e-06


def padded(block, sides, width):
    for axis, dim in sides:
        count = lax.axis_size(axis)
        forward = [(i, i + 1) for i in range(count - 1)]
        backward = [(target, source) for source, target in forward]
        low = lax.ppermute(
            lax.slice_in_dim(block, block.shape[dim] - width, None, axis=dim), axis, forward
        )
        high = lax.ppermute(lax.slice_in_dim(block, 0, width, axis=dim), axis, backward)
        block = jnp.concatenate([low, block, high], axis=dim)
    return block


def box_coords(box_pos):
    box_count = box_pos.shape[0]
    slab_coord = (jnp.arange(box_count, dtype=jnp.int32) // (CY * CZ)).astype(jnp.float32)
    row_coord = (box_pos // CZ).astype(jnp.float32)
    col_coord = (box_pos % CZ).astype(jnp.float32)
    return (slab_coord, row_coord, col_coord)


def translator(column, targets, coords):
    slab_gap = targets[0][:, None] - coords[0][None, :]
    row_gap = targets[1][:, None] - coords[1][None, :]
    col_gap = targets[2][:, None] - coords[2][None, :]
    square = slab_gap * slab_gap + row_gap * row_gap + col_gap * col_gap
    nearby = jnp.maximum(jnp.maximum(jnp.abs(slab_gap), jnp.abs(row_gap)), jnp.abs(col_gap)) < 1.5
    radius = jnp.sqrt(jnp.maximum(square, 1.0))
    kappa = wave_number * BSIDE
    argument = kappa * radius
    inverse = 1.0 / argument
    cosine = (column[0] * slab_gap + column[1] * row_gap + column[2] * col_gap) / radius
    prev_re, prev_im = (inverse, jnp.zeros_like(inverse))
    now_re, now_im = (jnp.zeros_like(inverse), -inverse)
    leg_prev, leg_now = (jnp.ones_like(inverse), jnp.ones_like(inverse))
    total_re = jnp.zeros_like(inverse)
    total_im = jnp.zeros_like(inverse)
    for order in range(4):
        if order == 0:
            legendre = jnp.ones_like(inverse)
        elif order == 1:
            legendre = cosine
        else:
            legendre = ((2 * order - 1) * cosine * leg_now - (order - 1) * leg_prev) / order
        leg_prev, leg_now = (leg_now, legendre)
        weight = (2.0 * order + 1.0) * legendre
        rot = order % 4
        if rot == 0:
            term_re, term_im = (now_re, now_im)
        elif rot == 1:
            term_re, term_im = (-now_im, now_re)
        elif rot == 2:
            term_re, term_im = (-now_re, -now_im)
        else:
            term_re, term_im = (now_im, -now_re)
        total_re = total_re + weight * term_re
        total_im = total_im + weight * term_im
        next_re = (2.0 * order + 1.0) * inverse * now_re - prev_re
        next_im = (2.0 * order + 1.0) * inverse * now_im - prev_im
        prev_re, prev_im = (now_re, now_im)
        now_re, now_im = (next_re, next_im)
    wave_re = jnp.cos(argument)
    wave_im = jnp.sin(argument)
    factor = jnp.where(nearby, 0.0, far_scale * kappa / 16.0)
    real_part = factor * (total_re * wave_re - total_im * wave_im)
    imag_part = factor * (total_re * wave_im + total_im * wave_re)
    return jnp.stack([real_part, imag_part]).astype(jnp.bfloat16)


def build_translators(columns, box_pos, box_dev):
    coords = box_coords(box_pos)
    first = lax.axis_index("box") * box_dev
    targets = tuple(lax.dynamic_slice_in_dim(part, first, box_dev) for part in coords)

    def one_direction(column):
        return translator(column, targets, coords)

    return jax.vmap(one_direction)(columns)


def green_constants():
    index = np.arange(V)
    coords = np.stack([index // (BSIDE * BSIDE), index // BSIDE % BSIDE, index % BSIDE])
    blocks = []
    for base in range(8):
        offset = (base // 4, base // 2 % 2, base % 2)
        square = np.zeros((V, V), np.float64)
        for dimension in range(3):
            differ = coords[dimension][:, None] - coords[dimension][None, :] - BSIDE * offset[dimension]
            square = square + differ * differ
        radius = np.sqrt(np.maximum(square, 1.0))
        inside = square < 0.5
        real_part = np.where(inside, self_value, near_scale * np.cos(wave_number * radius) / radius)
        imag_part = np.where(inside, 0.0, near_scale * np.sin(wave_number * radius) / radius)
        blocks.append(np.concatenate([real_part, imag_part], axis=0))
    return np.stack(blocks).astype(np.float32)


def pair_tables():
    slab_of, pos_of, valid, flips = [], [], [], []
    for base in range(8):
        bx, by, bz = base // 4, base // 2 % 2, base % 2
        for target in range(CY * CZ):
            ty, tz = target // CZ, target % CZ
            for side in range(2):
                shift_x = 0 if bx == 0 else (1 if side == 0 else -1)
                slab_of.append(1 + shift_x)
                pos_of.append((ty ^ by) * CZ + (tz ^ bz))
                valid.append(1.0 if (bx == 1 or side == 0) else 0.0)
                flips.append((shift_x < 0, by == 1 and ty == 1, bz == 1 and tz == 1))
    return (np.array(slab_of), np.array(pos_of), np.array(valid, np.float32), np.array(flips))


def flip_matrices():
    index = np.arange(V)
    coords = [index // (BSIDE * BSIDE), index // BSIDE % BSIDE, index % BSIDE]
    matrices = []
    for dimension in range(3):
        moved = list(coords)
        moved[dimension] = BSIDE - 1 - coords[dimension]
        source = moved[0] * BSIDE * BSIDE + moved[1] * BSIDE + moved[2]
        matrices.append((source[None, :] == index[:, None]).astype(np.float32))
    return matrices


def masked_flips(rows, masks, precision):
    for matrix, mask in zip(flip_matrices(), masks):
        flipped = jnp.dot(
            rows, jnp.asarray(matrix, rows.dtype), precision=precision,
            preferred_element_type=jnp.float32,
        ).astype(rows.dtype)
        rows = jnp.where(mask[:, None], flipped, rows)
    return rows


def near_field(sources, box_pos):
    exc_dev = sources.shape[1]
    box_dev = sources.shape[2]
    slots = CY * CZ
    extended = padded(sources, (("box", 2),), box_dev)
    zeros_pos = jnp.zeros((box_dev,), jnp.int32)
    padded_pos = jnp.concatenate([zeros_pos, box_pos, zeros_pos])
    local_pos = lax.dynamic_slice_in_dim(padded_pos, lax.axis_index("box") * box_dev, 3 * box_dev)
    slab_of, pos_of, valid, flips = pair_tables()
    column_slab = np.arange(3 * box_dev) // box_dev
    selector = (
        (slab_of[:, None] == column_slab[None, :])
        & (pos_of[:, None] == local_pos[None, :])
    ).astype(jnp.float32) * valid[:, None]
    selector = selector.reshape(8, 1, slots, 2, 1, 1, 1, 3 * box_dev)
    part_eye = np.eye(2, dtype=np.float32).reshape(1, 2, 1, 1, 1, 2, 1, 1)
    exc_eye = np.eye(exc_dev, dtype=np.float32).reshape(1, 1, 1, 1, exc_dev, 1, exc_dev, 1)
    gather = (selector * part_eye * exc_eye).reshape(-1, 2 * exc_dev * 3 * box_dev)
    pieces = jnp.dot(
        gather.astype(jnp.bfloat16), extended.reshape(-1, V), preferred_element_type=jnp.float32
    ).astype(jnp.bfloat16)
    row_flips = np.broadcast_to(
        flips.reshape(8, 1, slots, 2, 1, 3), (8, 2, slots, 2, exc_dev, 3)
    ).reshape(-1, 3)
    masks = [row_flips[:, d] for d in range(3)]
    pieces = masked_flips(pieces, masks, None)
    blocks = jnp.asarray(green_constants(), jnp.bfloat16)
    product = lax.dot_general(
        pieces.reshape(8, -1, V), blocks, (((2,), (2,)), ((0,), (0,))),
        preferred_element_type=jnp.float32,
    )
    product = product.reshape(8, 2, -1, 2, V)
    result = jnp.stack(
        [
            product[:, 0, :, 0] - product[:, 1, :, 1],
            product[:, 0, :, 1] + product[:, 1, :, 0],
        ],
        axis=1,
    ).reshape(-1, V)
    result = masked_flips(result, masks, lax.Precision.HIGHEST)
    own_pos = local_pos[box_dev : 2 * box_dev]
    choose = (own_pos[:, None] == jnp.arange(slots, dtype=jnp.int32)[None, :]).astype(jnp.float32)
    choose = choose.reshape(1, 1, box_dev, 1, 1, slots, 1, 1)
    part_eye = np.eye(2, dtype=np.float32).reshape(2, 1, 1, 1, 2, 1, 1, 1)
    exc_eye = np.eye(exc_dev, dtype=np.float32).reshape(1, exc_dev, 1, 1, 1, 1, 1, exc_dev)
    ones = np.ones((1, 1, 1, 8, 1, 1, 2, 1), np.float32)
    summing = (choose * part_eye * exc_eye * ones).reshape(2 * exc_dev * box_dev, -1)
    placed = jnp.dot(summing, result, precision=lax.Precision.HIGHEST)
    return placed.reshape(2, exc_dev, box_dev, V)


def encode(sources, enc_table):
    real_prod = jnp.einsum(
        "kv,xebv->kxeb", enc_table[0], sources, preferred_element_type=jnp.float32
    )
    imag_prod = jnp.einsum(
        "kv,xebv->kxeb", enc_table[1], sources, preferred_element_type=jnp.float32
    )
    return jnp.stack(
        [real_prod[:, 0] - imag_prod[:, 1], imag_prod[:, 0] + real_prod[:, 1]], axis=1
    ).astype(jnp.bfloat16)


def translate(encoded, translators):
    real_prod = jnp.einsum(
        "kts,skxe->kxet", translators[:, 0], encoded, preferred_element_type=jnp.float32
    )
    imag_prod = jnp.einsum(
        "kts,skxe->kxet", translators[:, 1], encoded, preferred_element_type=jnp.float32
    )
    return jnp.stack(
        [real_prod[:, 0] - imag_prod[:, 1], imag_prod[:, 0] + real_prod[:, 1]], axis=1
    ).astype(jnp.bfloat16)


def decode(returned, dec_table):
    real_prod = jnp.einsum(
        "vk,kxeb->xebv", dec_table[0], returned, preferred_element_type=jnp.float32
    )
    imag_prod = jnp.einsum(
        "vk,kxeb->xebv", dec_table[1], returned, preferred_element_type=jnp.float32
    )
    return jnp.stack([real_prod[0] - imag_prod[1], imag_prod[0] + real_prod[1]])


def shards(incident, contrast, box_pos, directions, enc_table, dec_table):
    contrast_real = contrast.astype(jnp.float32) * chi_step
    columns = lax.all_gather(jnp.transpose(directions), "box", axis=0, tiled=True)
    translators = build_translators(columns, box_pos, contrast.shape[0])
    fields = incident
    outputs = []
    for term_index in range(2):
        sources = (contrast_real[None, None] * fields.astype(jnp.float32)).astype(jnp.bfloat16)
        near_part = near_field(sources, box_pos)
        encoded = encode(sources, enc_table)
        by_box = jnp.transpose(encoded, (3, 0, 1, 2))
        gathered = lax.all_gather(by_box, "box", axis=0, tiled=True)
        returned = translate(gathered, translators)
        fields = (near_part + decode(returned, dec_table)).astype(jnp.bfloat16)
        outputs.append(fields)
    first_sq = jnp.sum(jnp.square(outputs[0].astype(jnp.float32)), axis=(0, 1, 3))
    second_sq = jnp.sum(jnp.square(outputs[1].astype(jnp.float32)), axis=(0, 1, 3))
    first_sum, second_sum = lax.psum((first_sq, second_sq), "exc")
    entry_count = 2 * outputs[0].shape[1] * lax.axis_size("exc") * outputs[0].shape[3]
    series_ratio = jnp.sqrt(second_sum / entry_count / (first_sum / entry_count + epsilon))
    return (outputs[0], outputs[1], series_ratio)


def solution(mesh):
    placed = (P(None, "exc", "box", None), P("box", None), P(), P(None, "box"), P(), P())
    return jax.shard_map(
        shards,
        mesh=mesh,
        in_specs=placed,
        out_specs=(P(None, "exc", "box", None), P(None, "exc", "box", None), P("box")),
        check_vma=False,
    )
```

```python
import numpy as np
import jax
import jax.numpy as jnp
from jax import lax
from jax.sharding import PartitionSpec as P

BSIDE = 8
CY = 2
CZ = 2
V = 512


wave_number = 0.8
near_scale = 0.1
self_value = 1.0
far_scale = 0.25
chi_step = 0.0625
epsilon = 1e-06


def padded(block, sides, width):
    for axis, dim in sides:
        count = lax.axis_size(axis)
        forward = [(i, i + 1) for i in range(count - 1)]
        backward = [(target, source) for source, target in forward]
        low = lax.ppermute(
            lax.slice_in_dim(block, block.shape[dim] - width, None, axis=dim), axis, forward
        )
        high = lax.ppermute(lax.slice_in_dim(block, 0, width, axis=dim), axis, backward)
        block = jnp.concatenate([low, block, high], axis=dim)
    return block


def box_coords(box_pos):
    box_count = box_pos.shape[0]
    slab_coord = (jnp.arange(box_count, dtype=jnp.int32) // (CY * CZ)).astype(jnp.float32)
    row_coord = (box_pos // CZ).astype(jnp.float32)
    col_coord = (box_pos % CZ).astype(jnp.float32)
    return (slab_coord, row_coord, col_coord)


def translator(column, coords):
    slab_gap = coords[0][:, None] - coords[0][None, :]
    row_gap = coords[1][:, None] - coords[1][None, :]
    col_gap = coords[2][:, None] - coords[2][None, :]
    square = slab_gap * slab_gap + row_gap * row_gap + col_gap * col_gap
    nearby = jnp.maximum(jnp.maximum(jnp.abs(slab_gap), jnp.abs(row_gap)), jnp.abs(col_gap)) < 1.5
    radius = jnp.sqrt(jnp.maximum(square, 1.0))
    kappa = wave_number * BSIDE
    argument = kappa * radius
    inverse = 1.0 / argument
    cosine = (column[0] * slab_gap + column[1] * row_gap + column[2] * col_gap) / radius
    prev_re, prev_im = (inverse, jnp.zeros_like(inverse))
    now_re, now_im = (jnp.zeros_like(inverse), -inverse)
    leg_prev, leg_now = (jnp.ones_like(inverse), jnp.ones_like(inverse))
    total_re = jnp.zeros_like(inverse)
    total_im = jnp.zeros_like(inverse)
    for order in range(4):
        if order == 0:
            legendre = jnp.ones_like(inverse)
        elif order == 1:
            legendre = cosine
        else:
            legendre = ((2 * order - 1) * cosine * leg_now - (order - 1) * leg_prev) / order
        leg_prev, leg_now = (leg_now, legendre)
        weight = (2.0 * order + 1.0) * legendre
        rot = order % 4
        if rot == 0:
            term_re, term_im = (now_re, now_im)
        elif rot == 1:
            term_re, term_im = (-now_im, now_re)
        elif rot == 2:
            term_re, term_im = (-now_re, -now_im)
        else:
            term_re, term_im = (now_im, -now_re)
        total_re = total_re + weight * term_re
        total_im = total_im + weight * term_im
        next_re = (2.0 * order + 1.0) * inverse * now_re - prev_re
        next_im = (2.0 * order + 1.0) * inverse * now_im - prev_im
        prev_re, prev_im = (now_re, now_im)
        now_re, now_im = (next_re, next_im)
    wave_re = jnp.cos(argument)
    wave_im = jnp.sin(argument)
    factor = jnp.where(nearby, 0.0, far_scale * kappa / 16.0)
    real_part = factor * (total_re * wave_re - total_im * wave_im)
    imag_part = factor * (total_re * wave_im + total_im * wave_re)
    return jnp.stack([real_part, imag_part]).astype(jnp.bfloat16)


def build_translators(dir_block, box_pos):
    coords = box_coords(box_pos)

    def one_direction(column):
        return translator(column, coords)

    return jax.vmap(one_direction)(jnp.transpose(dir_block))


def green_constants():
    index = np.arange(V)
    coords = np.stack([index // (BSIDE * BSIDE), index // BSIDE % BSIDE, index % BSIDE])
    blocks = []
    for base in range(8):
        offset = (base // 4, base // 2 % 2, base % 2)
        square = np.zeros((V, V), np.float64)
        for dimension in range(3):
            differ = coords[dimension][:, None] - coords[dimension][None, :] - BSIDE * offset[dimension]
            square = square + differ * differ
        radius = np.sqrt(np.maximum(square, 1.0))
        inside = square < 0.5
        real_part = np.where(inside, self_value, near_scale * np.cos(wave_number * radius) / radius)
        imag_part = np.where(inside, 0.0, near_scale * np.sin(wave_number * radius) / radius)
        blocks.append(np.concatenate([real_part, imag_part], axis=0))
    return np.stack(blocks).astype(np.float32)


def pair_tables():
    slab_of, pos_of, valid, flips = [], [], [], []
    for base in range(8):
        bx, by, bz = base // 4, base // 2 % 2, base % 2
        for target in range(CY * CZ):
            ty, tz = target // CZ, target % CZ
            for side in range(2):
                shift_x = 0 if bx == 0 else (1 if side == 0 else -1)
                slab_of.append(1 + shift_x)
                pos_of.append((ty ^ by) * CZ + (tz ^ bz))
                valid.append(1.0 if (bx == 1 or side == 0) else 0.0)
                flips.append((shift_x < 0, by == 1 and ty == 1, bz == 1 and tz == 1))
    return (np.array(slab_of), np.array(pos_of), np.array(valid, np.float32), np.array(flips))


def flip_matrices():
    index = np.arange(V)
    coords = [index // (BSIDE * BSIDE), index // BSIDE % BSIDE, index % BSIDE]
    matrices = []
    for dimension in range(3):
        moved = list(coords)
        moved[dimension] = BSIDE - 1 - coords[dimension]
        source = moved[0] * BSIDE * BSIDE + moved[1] * BSIDE + moved[2]
        matrices.append((source[None, :] == index[:, None]).astype(np.float32))
    return matrices


def masked_flips(rows, masks, precision):
    for matrix, mask in zip(flip_matrices(), masks):
        flipped = jnp.dot(
            rows, jnp.asarray(matrix, rows.dtype), precision=precision,
            preferred_element_type=jnp.float32,
        ).astype(rows.dtype)
        rows = jnp.where(mask[:, None], flipped, rows)
    return rows


def near_field(sources, box_pos):
    exc_dev = sources.shape[1]
    box_dev = sources.shape[2]
    slots = CY * CZ
    extended = padded(sources, (("box", 2),), box_dev)
    zeros_pos = jnp.zeros((box_dev,), jnp.int32)
    padded_pos = jnp.concatenate([zeros_pos, box_pos, zeros_pos])
    local_pos = lax.dynamic_slice_in_dim(padded_pos, lax.axis_index("box") * box_dev, 3 * box_dev)
    slab_of, pos_of, valid, flips = pair_tables()
    column_slab = np.arange(3 * box_dev) // box_dev
    selector = (
        (slab_of[:, None] == column_slab[None, :])
        & (pos_of[:, None] == local_pos[None, :])
    ).astype(jnp.float32) * valid[:, None]
    selector = selector.reshape(8, 1, slots, 2, 1, 1, 1, 3 * box_dev)
    part_eye = np.eye(2, dtype=np.float32).reshape(1, 2, 1, 1, 1, 2, 1, 1)
    exc_eye = np.eye(exc_dev, dtype=np.float32).reshape(1, 1, 1, 1, exc_dev, 1, exc_dev, 1)
    gather = (selector * part_eye * exc_eye).reshape(-1, 2 * exc_dev * 3 * box_dev)
    pieces = jnp.dot(
        gather.astype(jnp.bfloat16), extended.reshape(-1, V), preferred_element_type=jnp.float32
    ).astype(jnp.bfloat16)
    row_flips = np.broadcast_to(
        flips.reshape(8, 1, slots, 2, 1, 3), (8, 2, slots, 2, exc_dev, 3)
    ).reshape(-1, 3)
    masks = [row_flips[:, d] for d in range(3)]
    pieces = masked_flips(pieces, masks, None)
    blocks = jnp.asarray(green_constants(), jnp.bfloat16)
    product = lax.dot_general(
        pieces.reshape(8, -1, V), blocks, (((2,), (2,)), ((0,), (0,))),
        preferred_element_type=jnp.float32,
    )
    product = product.reshape(8, 2, -1, 2, V)
    result = jnp.stack(
        [
            product[:, 0, :, 0] - product[:, 1, :, 1],
            product[:, 0, :, 1] + product[:, 1, :, 0],
        ],
        axis=1,
    ).reshape(-1, V)
    result = masked_flips(result, masks, lax.Precision.HIGHEST)
    own_pos = local_pos[box_dev : 2 * box_dev]
    choose = (own_pos[:, None] == jnp.arange(slots, dtype=jnp.int32)[None, :]).astype(jnp.float32)
    choose = choose.reshape(1, 1, box_dev, 1, 1, slots, 1, 1)
    part_eye = np.eye(2, dtype=np.float32).reshape(2, 1, 1, 1, 2, 1, 1, 1)
    exc_eye = np.eye(exc_dev, dtype=np.float32).reshape(1, exc_dev, 1, 1, 1, 1, 1, exc_dev)
    ones = np.ones((1, 1, 1, 8, 1, 1, 2, 1), np.float32)
    summing = (choose * part_eye * exc_eye * ones).reshape(2 * exc_dev * box_dev, -1)
    placed = jnp.dot(summing, result, precision=lax.Precision.HIGHEST)
    return placed.reshape(2, exc_dev, box_dev, V)


def encode(sources, enc_table):
    real_prod = jnp.einsum(
        "kv,xebv->kxeb", enc_table[0], sources, preferred_element_type=jnp.float32
    )
    imag_prod = jnp.einsum(
        "kv,xebv->kxeb", enc_table[1], sources, preferred_element_type=jnp.float32
    )
    return jnp.stack(
        [real_prod[:, 0] - imag_prod[:, 1], imag_prod[:, 0] + real_prod[:, 1]], axis=1
    ).astype(jnp.bfloat16)


def translate(encoded, translators):
    real_prod = jnp.einsum(
        "kts,kxes->kxet", translators[:, 0], encoded, preferred_element_type=jnp.float32
    )
    imag_prod = jnp.einsum(
        "kts,kxes->kxet", translators[:, 1], encoded, preferred_element_type=jnp.float32
    )
    return jnp.stack(
        [real_prod[:, 0] - imag_prod[:, 1], imag_prod[:, 0] + real_prod[:, 1]], axis=1
    ).astype(jnp.bfloat16)


def decode(returned, dec_table):
    real_prod = jnp.einsum(
        "vk,kxeb->xebv", dec_table[0], returned, preferred_element_type=jnp.float32
    )
    imag_prod = jnp.einsum(
        "vk,kxeb->xebv", dec_table[1], returned, preferred_element_type=jnp.float32
    )
    return jnp.stack([real_prod[0] - imag_prod[1], imag_prod[0] + real_prod[1]])


def shards(incident, contrast, box_pos, directions, enc_table, dec_table):
    contrast_real = contrast.astype(jnp.float32) * chi_step
    translators = build_translators(directions, box_pos)
    fields = incident
    outputs = []
    for term_index in range(2):
        sources = (contrast_real[None, None] * fields.astype(jnp.float32)).astype(jnp.bfloat16)
        encoded = encode(sources, enc_table)
        translated = translate(
            lax.all_to_all(encoded, "box", split_axis=0, concat_axis=3, tiled=True), translators
        )
        if term_index == 0:
            sources, translated = lax.optimization_barrier((sources, translated))
        near_part = near_field(sources, box_pos)
        returned = lax.all_to_all(translated, "box", split_axis=3, concat_axis=0, tiled=True)
        fields = (near_part + decode(returned, dec_table)).astype(jnp.bfloat16)
        outputs.append(fields)
    first_sq = jnp.sum(jnp.square(outputs[0].astype(jnp.float32)), axis=(0, 1, 3))
    second_sq = jnp.sum(jnp.square(outputs[1].astype(jnp.float32)), axis=(0, 1, 3))
    first_sum, second_sum = lax.psum((first_sq, second_sq), "exc")
    entry_count = 2 * outputs[0].shape[1] * lax.axis_size("exc") * outputs[0].shape[3]
    series_ratio = jnp.sqrt(second_sum / entry_count / (first_sum / entry_count + epsilon))
    return (outputs[0], outputs[1], series_ratio)


def solution(mesh):
    placed = (P(None, "exc", "box", None), P("box", None), P(), P(None, "box"), P(), P())
    return jax.shard_map(
        shards,
        mesh=mesh,
        in_specs=placed,
        out_specs=(P(None, "exc", "box", None), P(None, "exc", "box", None), P("box")),
        check_vma=False,
    )
```

```python
import numpy as np
import jax
import jax.numpy as jnp
from jax import lax
from jax.sharding import PartitionSpec as P

BSIDE = 8
CY = 2
CZ = 2
V = 512


wave_number = 0.8
near_scale = 0.1
self_value = 1.0
far_scale = 0.25
chi_step = 0.0625
epsilon = 1e-06


def padded(block, sides, width):
    for axis, dim in sides:
        count = lax.axis_size(axis)
        forward = [(i, i + 1) for i in range(count - 1)]
        backward = [(target, source) for source, target in forward]
        low = lax.ppermute(
            lax.slice_in_dim(block, block.shape[dim] - width, None, axis=dim), axis, forward
        )
        high = lax.ppermute(lax.slice_in_dim(block, 0, width, axis=dim), axis, backward)
        block = jnp.concatenate([low, block, high], axis=dim)
    return block


def box_coords(box_pos):
    box_count = box_pos.shape[0]
    slab_coord = (jnp.arange(box_count, dtype=jnp.int32) // (CY * CZ)).astype(jnp.float32)
    row_coord = (box_pos // CZ).astype(jnp.float32)
    col_coord = (box_pos % CZ).astype(jnp.float32)
    return (slab_coord, row_coord, col_coord)


def translator(column, coords):
    slab_gap = coords[0][:, None] - coords[0][None, :]
    row_gap = coords[1][:, None] - coords[1][None, :]
    col_gap = coords[2][:, None] - coords[2][None, :]
    square = slab_gap * slab_gap + row_gap * row_gap + col_gap * col_gap
    nearby = jnp.maximum(jnp.maximum(jnp.abs(slab_gap), jnp.abs(row_gap)), jnp.abs(col_gap)) < 1.5
    radius = jnp.sqrt(jnp.maximum(square, 1.0))
    kappa = wave_number * BSIDE
    argument = kappa * radius
    inverse = 1.0 / argument
    cosine = (column[0] * slab_gap + column[1] * row_gap + column[2] * col_gap) / radius
    prev_re, prev_im = (inverse, jnp.zeros_like(inverse))
    now_re, now_im = (jnp.zeros_like(inverse), -inverse)
    leg_prev, leg_now = (jnp.ones_like(inverse), jnp.ones_like(inverse))
    total_re = jnp.zeros_like(inverse)
    total_im = jnp.zeros_like(inverse)
    for order in range(4):
        if order == 0:
            legendre = jnp.ones_like(inverse)
        elif order == 1:
            legendre = cosine
        else:
            legendre = ((2 * order - 1) * cosine * leg_now - (order - 1) * leg_prev) / order
        leg_prev, leg_now = (leg_now, legendre)
        weight = (2.0 * order + 1.0) * legendre
        rot = order % 4
        if rot == 0:
            term_re, term_im = (now_re, now_im)
        elif rot == 1:
            term_re, term_im = (-now_im, now_re)
        elif rot == 2:
            term_re, term_im = (-now_re, -now_im)
        else:
            term_re, term_im = (now_im, -now_re)
        total_re = total_re + weight * term_re
        total_im = total_im + weight * term_im
        next_re = (2.0 * order + 1.0) * inverse * now_re - prev_re
        next_im = (2.0 * order + 1.0) * inverse * now_im - prev_im
        prev_re, prev_im = (now_re, now_im)
        now_re, now_im = (next_re, next_im)
    wave_re = jnp.cos(argument)
    wave_im = jnp.sin(argument)
    factor = jnp.where(nearby, 0.0, far_scale * kappa / 16.0)
    real_part = factor * (total_re * wave_re - total_im * wave_im)
    imag_part = factor * (total_re * wave_im + total_im * wave_re)
    return jnp.stack([real_part, imag_part]).astype(jnp.bfloat16)


def build_translators(dir_block, box_pos):
    coords = box_coords(box_pos)

    def one_direction(column):
        return translator(column, coords)

    return jax.vmap(one_direction)(jnp.transpose(dir_block))


def green_constants():
    index = np.arange(V)
    coords = np.stack([index // (BSIDE * BSIDE), index // BSIDE % BSIDE, index % BSIDE])
    blocks = []
    for base in range(8):
        offset = (base // 4, base // 2 % 2, base % 2)
        square = np.zeros((V, V), np.float64)
        for dimension in range(3):
            differ = coords[dimension][:, None] - coords[dimension][None, :] - BSIDE * offset[dimension]
            square = square + differ * differ
        radius = np.sqrt(np.maximum(square, 1.0))
        inside = square < 0.5
        real_part = np.where(inside, self_value, near_scale * np.cos(wave_number * radius) / radius)
        imag_part = np.where(inside, 0.0, near_scale * np.sin(wave_number * radius) / radius)
        blocks.append(np.concatenate([real_part, imag_part], axis=0))
    return np.stack(blocks).astype(np.float32)


def pair_tables():
    slab_of, pos_of, valid, flips = [], [], [], []
    for base in range(8):
        bx, by, bz = base // 4, base // 2 % 2, base % 2
        for target in range(CY * CZ):
            ty, tz = target // CZ, target % CZ
            for side in range(2):
                shift_x = 0 if bx == 0 else (1 if side == 0 else -1)
                slab_of.append(1 + shift_x)
                pos_of.append((ty ^ by) * CZ + (tz ^ bz))
                valid.append(1.0 if (bx == 1 or side == 0) else 0.0)
                flips.append((shift_x < 0, by == 1 and ty == 1, bz == 1 and tz == 1))
    return (np.array(slab_of), np.array(pos_of), np.array(valid, np.float32), np.array(flips))


def flip_matrices():
    index = np.arange(V)
    coords = [index // (BSIDE * BSIDE), index // BSIDE % BSIDE, index % BSIDE]
    matrices = []
    for dimension in range(3):
        moved = list(coords)
        moved[dimension] = BSIDE - 1 - coords[dimension]
        source = moved[0] * BSIDE * BSIDE + moved[1] * BSIDE + moved[2]
        matrices.append((source[None, :] == index[:, None]).astype(np.float32))
    return matrices


def masked_flips(rows, masks, precision):
    for matrix, mask in zip(flip_matrices(), masks):
        flipped = jnp.dot(
            rows, jnp.asarray(matrix, rows.dtype), precision=precision,
            preferred_element_type=jnp.float32,
        ).astype(rows.dtype)
        rows = jnp.where(mask[:, None], flipped, rows)
    return rows


def near_field(sources, box_pos):
    exc_dev = sources.shape[1]
    box_dev = sources.shape[2]
    slots = CY * CZ
    extended = padded(sources, (("box", 2),), box_dev)
    zeros_pos = jnp.zeros((box_dev,), jnp.int32)
    padded_pos = jnp.concatenate([zeros_pos, box_pos, zeros_pos])
    local_pos = lax.dynamic_slice_in_dim(padded_pos, lax.axis_index("box") * box_dev, 3 * box_dev)
    slab_of, pos_of, valid, flips = pair_tables()
    column_slab = np.arange(3 * box_dev) // box_dev
    selector = (
        (slab_of[:, None] == column_slab[None, :])
        & (pos_of[:, None] == local_pos[None, :])
    ).astype(jnp.float32) * valid[:, None]
    selector = selector.reshape(8, 1, slots, 2, 1, 1, 1, 3 * box_dev)
    part_eye = np.eye(2, dtype=np.float32).reshape(1, 2, 1, 1, 1, 2, 1, 1)
    exc_eye = np.eye(exc_dev, dtype=np.float32).reshape(1, 1, 1, 1, exc_dev, 1, exc_dev, 1)
    gather = (selector * part_eye * exc_eye).reshape(-1, 2 * exc_dev * 3 * box_dev)
    pieces = jnp.dot(
        gather.astype(jnp.bfloat16), extended.reshape(-1, V), preferred_element_type=jnp.float32
    ).astype(jnp.bfloat16)
    row_flips = np.broadcast_to(
        flips.reshape(8, 1, slots, 2, 1, 3), (8, 2, slots, 2, exc_dev, 3)
    ).reshape(-1, 3)
    masks = [row_flips[:, d] for d in range(3)]
    pieces = masked_flips(pieces, masks, None)
    blocks = jnp.asarray(green_constants(), jnp.bfloat16)
    product = lax.dot_general(
        pieces.reshape(8, -1, V), blocks, (((2,), (2,)), ((0,), (0,))),
        preferred_element_type=jnp.float32,
    )
    product = product.reshape(8, 2, -1, 2, V)
    result = jnp.stack(
        [
            product[:, 0, :, 0] - product[:, 1, :, 1],
            product[:, 0, :, 1] + product[:, 1, :, 0],
        ],
        axis=1,
    ).reshape(-1, V)
    result = masked_flips(result, masks, lax.Precision.HIGHEST)
    own_pos = local_pos[box_dev : 2 * box_dev]
    choose = (own_pos[:, None] == jnp.arange(slots, dtype=jnp.int32)[None, :]).astype(jnp.float32)
    choose = choose.reshape(1, 1, box_dev, 1, 1, slots, 1, 1)
    part_eye = np.eye(2, dtype=np.float32).reshape(2, 1, 1, 1, 2, 1, 1, 1)
    exc_eye = np.eye(exc_dev, dtype=np.float32).reshape(1, exc_dev, 1, 1, 1, 1, 1, exc_dev)
    ones = np.ones((1, 1, 1, 8, 1, 1, 2, 1), np.float32)
    summing = (choose * part_eye * exc_eye * ones).reshape(2 * exc_dev * box_dev, -1)
    placed = jnp.dot(summing, result, precision=lax.Precision.HIGHEST)
    return placed.reshape(2, exc_dev, box_dev, V)


def encode(sources, enc_table):
    real_prod = jnp.einsum(
        "kv,xebv->kxeb", enc_table[0], sources, preferred_element_type=jnp.float32
    )
    imag_prod = jnp.einsum(
        "kv,xebv->kxeb", enc_table[1], sources, preferred_element_type=jnp.float32
    )
    return jnp.stack(
        [real_prod[:, 0] - imag_prod[:, 1], imag_prod[:, 0] + real_prod[:, 1]], axis=1
    ).astype(jnp.bfloat16)


def translate(encoded, translators):
    real_prod = jnp.einsum(
        "kts,kxes->kxet", translators[:, 0], encoded, preferred_element_type=jnp.float32
    )
    imag_prod = jnp.einsum(
        "kts,kxes->kxet", translators[:, 1], encoded, preferred_element_type=jnp.float32
    )
    return jnp.stack(
        [real_prod[:, 0] - imag_prod[:, 1], imag_prod[:, 0] + real_prod[:, 1]], axis=1
    ).astype(jnp.bfloat16)


def decode(returned, dec_table):
    real_prod = jnp.einsum(
        "vk,kxeb->xebv", dec_table[0], returned, preferred_element_type=jnp.float32
    )
    imag_prod = jnp.einsum(
        "vk,kxeb->xebv", dec_table[1], returned, preferred_element_type=jnp.float32
    )
    return jnp.stack([real_prod[0] - imag_prod[1], imag_prod[0] + real_prod[1]])


def shards(incident, contrast, box_pos, directions, enc_table, dec_table):
    contrast_real = contrast.astype(jnp.float32) * chi_step
    translators = build_translators(directions, box_pos)
    fields = incident
    outputs = []
    for term_index in range(2):
        sources = (contrast_real[None, None] * fields.astype(jnp.float32)).astype(jnp.bfloat16)
        encoded = encode(sources, enc_table)
        translated = translate(
            lax.all_to_all(encoded, "box", split_axis=0, concat_axis=3, tiled=True), translators
        )
        sources, translated = lax.optimization_barrier((sources, translated))
        near_part = near_field(sources, box_pos)
        returned = lax.all_to_all(translated, "box", split_axis=3, concat_axis=0, tiled=True)
        fields = (near_part + decode(returned, dec_table)).astype(jnp.bfloat16)
        outputs.append(fields)
    first_sq = jnp.sum(jnp.square(outputs[0].astype(jnp.float32)), axis=(0, 1, 3))
    second_sq = jnp.sum(jnp.square(outputs[1].astype(jnp.float32)), axis=(0, 1, 3))
    first_sum, second_sum = lax.psum((first_sq, second_sq), "exc")
    entry_count = 2 * outputs[0].shape[1] * lax.axis_size("exc") * outputs[0].shape[3]
    series_ratio = jnp.sqrt(second_sum / entry_count / (first_sum / entry_count + epsilon))
    return (outputs[0], outputs[1], series_ratio)


def solution(mesh):
    placed = (P(None, "exc", "box", None), P("box", None), P(), P(None, "box"), P(), P())
    return jax.shard_map(
        shards,
        mesh=mesh,
        in_specs=placed,
        out_specs=(P(None, "exc", "box", None), P(None, "exc", "box", None), P("box")),
        check_vma=False,
    )
```

```python
import numpy as np
import jax
import jax.numpy as jnp
from jax import lax
from jax.sharding import PartitionSpec as P

BSIDE = 8
CY = 2
CZ = 2
V = 512


wave_number = 0.8
near_scale = 0.1
self_value = 1.0
far_scale = 0.25
chi_step = 0.0625
epsilon = 1e-06


def padded(block, sides, width):
    for axis, dim in sides:
        count = lax.axis_size(axis)
        forward = [(i, i + 1) for i in range(count - 1)]
        backward = [(target, source) for source, target in forward]
        low = lax.ppermute(
            lax.slice_in_dim(block, block.shape[dim] - width, None, axis=dim), axis, forward
        )
        high = lax.ppermute(lax.slice_in_dim(block, 0, width, axis=dim), axis, backward)
        block = jnp.concatenate([low, block, high], axis=dim)
    return block


def box_coords(box_pos):
    box_count = box_pos.shape[0]
    slab_coord = (jnp.arange(box_count, dtype=jnp.int32) // (CY * CZ)).astype(jnp.float32)
    row_coord = (box_pos // CZ).astype(jnp.float32)
    col_coord = (box_pos % CZ).astype(jnp.float32)
    return (slab_coord, row_coord, col_coord)


def translator(column, coords):
    slab_gap = coords[0][:, None] - coords[0][None, :]
    row_gap = coords[1][:, None] - coords[1][None, :]
    col_gap = coords[2][:, None] - coords[2][None, :]
    square = slab_gap * slab_gap + row_gap * row_gap + col_gap * col_gap
    nearby = jnp.maximum(jnp.maximum(jnp.abs(slab_gap), jnp.abs(row_gap)), jnp.abs(col_gap)) < 1.5
    radius = jnp.sqrt(jnp.maximum(square, 1.0))
    kappa = wave_number * BSIDE
    argument = kappa * radius
    inverse = 1.0 / argument
    cosine = (column[0] * slab_gap + column[1] * row_gap + column[2] * col_gap) / radius
    prev_re, prev_im = (inverse, jnp.zeros_like(inverse))
    now_re, now_im = (jnp.zeros_like(inverse), -inverse)
    leg_prev, leg_now = (jnp.ones_like(inverse), jnp.ones_like(inverse))
    total_re = jnp.zeros_like(inverse)
    total_im = jnp.zeros_like(inverse)
    for order in range(4):
        if order == 0:
            legendre = jnp.ones_like(inverse)
        elif order == 1:
            legendre = cosine
        else:
            legendre = ((2 * order - 1) * cosine * leg_now - (order - 1) * leg_prev) / order
        leg_prev, leg_now = (leg_now, legendre)
        weight = (2.0 * order + 1.0) * legendre
        rot = order % 4
        if rot == 0:
            term_re, term_im = (now_re, now_im)
        elif rot == 1:
            term_re, term_im = (-now_im, now_re)
        elif rot == 2:
            term_re, term_im = (-now_re, -now_im)
        else:
            term_re, term_im = (now_im, -now_re)
        total_re = total_re + weight * term_re
        total_im = total_im + weight * term_im
        next_re = (2.0 * order + 1.0) * inverse * now_re - prev_re
        next_im = (2.0 * order + 1.0) * inverse * now_im - prev_im
        prev_re, prev_im = (now_re, now_im)
        now_re, now_im = (next_re, next_im)
    wave_re = jnp.cos(argument)
    wave_im = jnp.sin(argument)
    factor = jnp.where(nearby, 0.0, far_scale * kappa / 16.0)
    real_part = factor * (total_re * wave_re - total_im * wave_im)
    imag_part = factor * (total_re * wave_im + total_im * wave_re)
    return jnp.stack([real_part, imag_part]).astype(jnp.bfloat16)


def build_translators(dir_block, box_pos):
    coords = box_coords(box_pos)

    def one_direction(column):
        return translator(column, coords)

    return jax.vmap(one_direction)(jnp.transpose(dir_block))


def green_constants():
    index = np.arange(V)
    coords = np.stack([index // (BSIDE * BSIDE), index // BSIDE % BSIDE, index % BSIDE])
    blocks = []
    for base in range(8):
        offset = (base // 4, base // 2 % 2, base % 2)
        square = np.zeros((V, V), np.float64)
        for dimension in range(3):
            differ = coords[dimension][:, None] - coords[dimension][None, :] - BSIDE * offset[dimension]
            square = square + differ * differ
        radius = np.sqrt(np.maximum(square, 1.0))
        inside = square < 0.5
        real_part = np.where(inside, self_value, near_scale * np.cos(wave_number * radius) / radius)
        imag_part = np.where(inside, 0.0, near_scale * np.sin(wave_number * radius) / radius)
        blocks.append(np.concatenate([real_part, imag_part], axis=0))
    return np.stack(blocks).astype(np.float32)


def pair_tables():
    slab_of, pos_of, valid, flips = [], [], [], []
    for base in range(8):
        bx, by, bz = base // 4, base // 2 % 2, base % 2
        for target in range(CY * CZ):
            ty, tz = target // CZ, target % CZ
            for side in range(2):
                shift_x = 0 if bx == 0 else (1 if side == 0 else -1)
                slab_of.append(1 + shift_x)
                pos_of.append((ty ^ by) * CZ + (tz ^ bz))
                valid.append(1.0 if (bx == 1 or side == 0) else 0.0)
                flips.append((shift_x < 0, by == 1 and ty == 1, bz == 1 and tz == 1))
    return (np.array(slab_of), np.array(pos_of), np.array(valid, np.float32), np.array(flips))


def flip_matrices():
    index = np.arange(V)
    coords = [index // (BSIDE * BSIDE), index // BSIDE % BSIDE, index % BSIDE]
    matrices = []
    for dimension in range(3):
        moved = list(coords)
        moved[dimension] = BSIDE - 1 - coords[dimension]
        source = moved[0] * BSIDE * BSIDE + moved[1] * BSIDE + moved[2]
        matrices.append((source[None, :] == index[:, None]).astype(np.float32))
    return matrices


def masked_flips(rows, masks, precision):
    for matrix, mask in zip(flip_matrices(), masks):
        flipped = jnp.dot(
            rows, jnp.asarray(matrix, rows.dtype), precision=precision,
            preferred_element_type=jnp.float32,
        ).astype(rows.dtype)
        rows = jnp.where(mask[:, None], flipped, rows)
    return rows


def near_field(sources, box_pos):
    exc_dev = sources.shape[1]
    box_dev = sources.shape[2]
    slots = CY * CZ
    extended = padded(sources, (("box", 2),), box_dev)
    zeros_pos = jnp.zeros((box_dev,), jnp.int32)
    padded_pos = jnp.concatenate([zeros_pos, box_pos, zeros_pos])
    local_pos = lax.dynamic_slice_in_dim(padded_pos, lax.axis_index("box") * box_dev, 3 * box_dev)
    slab_of, pos_of, valid, flips = pair_tables()
    column_slab = np.arange(3 * box_dev) // box_dev
    selector = (
        (slab_of[:, None] == column_slab[None, :])
        & (pos_of[:, None] == local_pos[None, :])
    ).astype(jnp.float32) * valid[:, None]
    selector = selector.reshape(8, 1, slots, 2, 1, 1, 1, 3 * box_dev)
    part_eye = np.eye(2, dtype=np.float32).reshape(1, 2, 1, 1, 1, 2, 1, 1)
    exc_eye = np.eye(exc_dev, dtype=np.float32).reshape(1, 1, 1, 1, exc_dev, 1, exc_dev, 1)
    gather = (selector * part_eye * exc_eye).reshape(-1, 2 * exc_dev * 3 * box_dev)
    pieces = jnp.dot(
        gather.astype(jnp.bfloat16), extended.reshape(-1, V), preferred_element_type=jnp.float32
    ).astype(jnp.bfloat16)
    row_flips = np.broadcast_to(
        flips.reshape(8, 1, slots, 2, 1, 3), (8, 2, slots, 2, exc_dev, 3)
    ).reshape(-1, 3)
    masks = [row_flips[:, d] for d in range(3)]
    pieces = masked_flips(pieces, masks, None)
    blocks = jnp.asarray(green_constants(), jnp.bfloat16)
    product = lax.dot_general(
        pieces.reshape(8, -1, V), blocks, (((2,), (2,)), ((0,), (0,))),
        preferred_element_type=jnp.float32,
    )
    product = product.reshape(8, 2, -1, 2, V)
    result = jnp.stack(
        [
            product[:, 0, :, 0] - product[:, 1, :, 1],
            product[:, 0, :, 1] + product[:, 1, :, 0],
        ],
        axis=1,
    ).reshape(-1, V)
    result = masked_flips(result, masks, lax.Precision.HIGHEST)
    own_pos = local_pos[box_dev : 2 * box_dev]
    choose = (own_pos[:, None] == jnp.arange(slots, dtype=jnp.int32)[None, :]).astype(jnp.float32)
    choose = choose.reshape(1, 1, box_dev, 1, 1, slots, 1, 1)
    part_eye = np.eye(2, dtype=np.float32).reshape(2, 1, 1, 1, 2, 1, 1, 1)
    exc_eye = np.eye(exc_dev, dtype=np.float32).reshape(1, exc_dev, 1, 1, 1, 1, 1, exc_dev)
    ones = np.ones((1, 1, 1, 8, 1, 1, 2, 1), np.float32)
    summing = (choose * part_eye * exc_eye * ones).reshape(2 * exc_dev * box_dev, -1)
    placed = jnp.dot(summing, result, precision=lax.Precision.HIGHEST)
    return placed.reshape(2, exc_dev, box_dev, V)


def encode(sources, enc_table):
    real_prod = jnp.einsum(
        "kv,xebv->kxeb", enc_table[0], sources, preferred_element_type=jnp.float32
    )
    imag_prod = jnp.einsum(
        "kv,xebv->kxeb", enc_table[1], sources, preferred_element_type=jnp.float32
    )
    return jnp.stack(
        [real_prod[:, 0] - imag_prod[:, 1], imag_prod[:, 0] + real_prod[:, 1]], axis=1
    ).astype(jnp.bfloat16)


def translate(encoded, translators):
    product = jnp.einsum(
        "kcts,kxes->kcxet", translators, encoded, preferred_element_type=jnp.float32
    )
    return jnp.stack(
        [product[:, 0, 0] - product[:, 1, 1], product[:, 1, 0] + product[:, 0, 1]], axis=1
    ).astype(jnp.bfloat16)


def decode(returned, dec_table):
    real_prod = jnp.einsum(
        "vk,kxeb->xebv", dec_table[0], returned, preferred_element_type=jnp.float32
    )
    imag_prod = jnp.einsum(
        "vk,kxeb->xebv", dec_table[1], returned, preferred_element_type=jnp.float32
    )
    return jnp.stack([real_prod[0] - imag_prod[1], imag_prod[0] + real_prod[1]])


def shards(incident, contrast, box_pos, directions, enc_table, dec_table):
    contrast_real = contrast.astype(jnp.float32) * chi_step
    translators = build_translators(directions, box_pos)
    fields = incident
    outputs = []
    for term_index in range(2):
        sources = (contrast_real[None, None] * fields.astype(jnp.float32)).astype(jnp.bfloat16)
        encoded = encode(sources, enc_table)
        translated = translate(
            lax.all_to_all(encoded, "box", split_axis=0, concat_axis=3, tiled=True), translators
        )
        sources, translated = lax.optimization_barrier((sources, translated))
        near_part = near_field(sources, box_pos)
        returned = lax.all_to_all(translated, "box", split_axis=3, concat_axis=0, tiled=True)
        fields = (near_part + decode(returned, dec_table)).astype(jnp.bfloat16)
        outputs.append(fields)
    first_sq = jnp.sum(jnp.square(outputs[0].astype(jnp.float32)), axis=(0, 1, 3))
    second_sq = jnp.sum(jnp.square(outputs[1].astype(jnp.float32)), axis=(0, 1, 3))
    first_sum, second_sum = lax.psum((first_sq, second_sq), "exc")
    entry_count = 2 * outputs[0].shape[1] * lax.axis_size("exc") * outputs[0].shape[3]
    series_ratio = jnp.sqrt(second_sum / entry_count / (first_sum / entry_count + epsilon))
    return (outputs[0], outputs[1], series_ratio)


def solution(mesh):
    placed = (P(None, "exc", "box", None), P("box", None), P(), P(None, "box"), P(), P())
    return jax.shard_map(
        shards,
        mesh=mesh,
        in_specs=placed,
        out_specs=(P(None, "exc", "box", None), P(None, "exc", "box", None), P("box")),
        check_vma=False,
    )
```

```python
import numpy as np
import jax
import jax.numpy as jnp
from jax import lax
from jax.sharding import PartitionSpec as P

BSIDE = 8
CY = 2
CZ = 2
V = 512


wave_number = 0.8
near_scale = 0.1
self_value = 1.0
far_scale = 0.25
chi_step = 0.0625
epsilon = 1e-06


def padded(block, sides, width):
    for axis, dim in sides:
        count = lax.axis_size(axis)
        forward = [(i, i + 1) for i in range(count - 1)]
        backward = [(target, source) for source, target in forward]
        low = lax.ppermute(
            lax.slice_in_dim(block, block.shape[dim] - width, None, axis=dim), axis, forward
        )
        high = lax.ppermute(lax.slice_in_dim(block, 0, width, axis=dim), axis, backward)
        block = jnp.concatenate([low, block, high], axis=dim)
    return block


def box_coords(box_pos):
    box_count = box_pos.shape[0]
    slab_coord = (jnp.arange(box_count, dtype=jnp.int32) // (CY * CZ)).astype(jnp.float32)
    row_coord = (box_pos // CZ).astype(jnp.float32)
    col_coord = (box_pos % CZ).astype(jnp.float32)
    return (slab_coord, row_coord, col_coord)


def translator(column, coords):
    slab_gap = coords[0][:, None] - coords[0][None, :]
    row_gap = coords[1][:, None] - coords[1][None, :]
    col_gap = coords[2][:, None] - coords[2][None, :]
    square = slab_gap * slab_gap + row_gap * row_gap + col_gap * col_gap
    nearby = jnp.maximum(jnp.maximum(jnp.abs(slab_gap), jnp.abs(row_gap)), jnp.abs(col_gap)) < 1.5
    radius = jnp.sqrt(jnp.maximum(square, 1.0))
    kappa = wave_number * BSIDE
    argument = kappa * radius
    inverse = 1.0 / argument
    cosine = (column[0] * slab_gap + column[1] * row_gap + column[2] * col_gap) / radius
    prev_re, prev_im = (inverse, jnp.zeros_like(inverse))
    now_re, now_im = (jnp.zeros_like(inverse), -inverse)
    leg_prev, leg_now = (jnp.ones_like(inverse), jnp.ones_like(inverse))
    total_re = jnp.zeros_like(inverse)
    total_im = jnp.zeros_like(inverse)
    for order in range(4):
        if order == 0:
            legendre = jnp.ones_like(inverse)
        elif order == 1:
            legendre = cosine
        else:
            legendre = ((2 * order - 1) * cosine * leg_now - (order - 1) * leg_prev) / order
        leg_prev, leg_now = (leg_now, legendre)
        weight = (2.0 * order + 1.0) * legendre
        rot = order % 4
        if rot == 0:
            term_re, term_im = (now_re, now_im)
        elif rot == 1:
            term_re, term_im = (-now_im, now_re)
        elif rot == 2:
            term_re, term_im = (-now_re, -now_im)
        else:
            term_re, term_im = (now_im, -now_re)
        total_re = total_re + weight * term_re
        total_im = total_im + weight * term_im
        next_re = (2.0 * order + 1.0) * inverse * now_re - prev_re
        next_im = (2.0 * order + 1.0) * inverse * now_im - prev_im
        prev_re, prev_im = (now_re, now_im)
        now_re, now_im = (next_re, next_im)
    wave_re = jnp.cos(argument)
    wave_im = jnp.sin(argument)
    factor = jnp.where(nearby, 0.0, far_scale * kappa / 16.0)
    real_part = factor * (total_re * wave_re - total_im * wave_im)
    imag_part = factor * (total_re * wave_im + total_im * wave_re)
    return jnp.stack([real_part, imag_part]).astype(jnp.bfloat16)


def build_translators(dir_block, box_pos):
    coords = box_coords(box_pos)

    def one_direction(column):
        return translator(column, coords)

    return jax.vmap(one_direction)(jnp.transpose(dir_block))


def green_constants():
    index = np.arange(V)
    coords = np.stack([index // (BSIDE * BSIDE), index // BSIDE % BSIDE, index % BSIDE])
    blocks = []
    for base in range(8):
        offset = (base // 4, base // 2 % 2, base % 2)
        square = np.zeros((V, V), np.float64)
        for dimension in range(3):
            differ = coords[dimension][:, None] - coords[dimension][None, :] - BSIDE * offset[dimension]
            square = square + differ * differ
        radius = np.sqrt(np.maximum(square, 1.0))
        inside = square < 0.5
        real_part = np.where(inside, self_value, near_scale * np.cos(wave_number * radius) / radius)
        imag_part = np.where(inside, 0.0, near_scale * np.sin(wave_number * radius) / radius)
        blocks.append(np.concatenate([real_part, imag_part], axis=0))
    return np.stack(blocks).astype(np.float32)


def pair_tables():
    slab_of, pos_of, valid, flips = [], [], [], []
    for base in range(8):
        bx, by, bz = base // 4, base // 2 % 2, base % 2
        for target in range(CY * CZ):
            ty, tz = target // CZ, target % CZ
            for side in range(2):
                shift_x = 0 if bx == 0 else (1 if side == 0 else -1)
                slab_of.append(1 + shift_x)
                pos_of.append((ty ^ by) * CZ + (tz ^ bz))
                valid.append(1.0 if (bx == 1 or side == 0) else 0.0)
                flips.append((shift_x < 0, by == 1 and ty == 1, bz == 1 and tz == 1))
    return (np.array(slab_of), np.array(pos_of), np.array(valid, np.float32), np.array(flips))


def flip_matrices():
    index = np.arange(V)
    coords = [index // (BSIDE * BSIDE), index // BSIDE % BSIDE, index % BSIDE]
    matrices = []
    for dimension in range(3):
        moved = list(coords)
        moved[dimension] = BSIDE - 1 - coords[dimension]
        source = moved[0] * BSIDE * BSIDE + moved[1] * BSIDE + moved[2]
        matrices.append((source[None, :] == index[:, None]).astype(np.float32))
    return matrices


def masked_flips(rows, masks, precision):
    for matrix, mask in zip(flip_matrices(), masks):
        flipped = jnp.dot(
            rows, jnp.asarray(matrix, rows.dtype), precision=precision,
            preferred_element_type=jnp.float32,
        ).astype(rows.dtype)
        rows = jnp.where(mask[:, None], flipped, rows)
    return rows


def near_field(sources, box_pos):
    exc_dev = sources.shape[1]
    box_dev = sources.shape[2]
    slots = CY * CZ
    extended = padded(sources, (("box", 2),), box_dev)
    zeros_pos = jnp.zeros((box_dev,), jnp.int32)
    padded_pos = jnp.concatenate([zeros_pos, box_pos, zeros_pos])
    local_pos = lax.dynamic_slice_in_dim(padded_pos, lax.axis_index("box") * box_dev, 3 * box_dev)
    slab_of, pos_of, valid, flips = pair_tables()
    column_slab = np.arange(3 * box_dev) // box_dev
    selector = (
        (slab_of[:, None] == column_slab[None, :])
        & (pos_of[:, None] == local_pos[None, :])
    ).astype(jnp.float32) * valid[:, None]
    selector = selector.reshape(8, 1, slots, 2, 1, 1, 1, 3 * box_dev)
    part_eye = np.eye(2, dtype=np.float32).reshape(1, 2, 1, 1, 1, 2, 1, 1)
    exc_eye = np.eye(exc_dev, dtype=np.float32).reshape(1, 1, 1, 1, exc_dev, 1, exc_dev, 1)
    gather = (selector * part_eye * exc_eye).reshape(-1, 2 * exc_dev * 3 * box_dev)
    pieces = jnp.dot(
        gather.astype(jnp.bfloat16), extended.reshape(-1, V), preferred_element_type=jnp.float32
    ).astype(jnp.bfloat16)
    row_flips = np.broadcast_to(
        flips.reshape(8, 1, slots, 2, 1, 3), (8, 2, slots, 2, exc_dev, 3)
    ).reshape(-1, 3)
    masks = [row_flips[:, d] for d in range(3)]
    pieces = masked_flips(pieces, masks, None)
    blocks = jnp.asarray(green_constants(), jnp.bfloat16)
    product = lax.dot_general(
        pieces.reshape(8, -1, V), blocks, (((2,), (2,)), ((0,), (0,))),
        preferred_element_type=jnp.float32,
    )
    product = product.reshape(8, 2, -1, 2, V)
    result = jnp.stack(
        [
            product[:, 0, :, 0] - product[:, 1, :, 1],
            product[:, 0, :, 1] + product[:, 1, :, 0],
        ],
        axis=1,
    ).reshape(-1, V)
    result = masked_flips(result, masks, lax.Precision.HIGHEST)
    own_pos = local_pos[box_dev : 2 * box_dev]
    choose = (own_pos[:, None] == jnp.arange(slots, dtype=jnp.int32)[None, :]).astype(jnp.float32)
    choose = choose.reshape(1, 1, box_dev, 1, 1, slots, 1, 1)
    part_eye = np.eye(2, dtype=np.float32).reshape(2, 1, 1, 1, 2, 1, 1, 1)
    exc_eye = np.eye(exc_dev, dtype=np.float32).reshape(1, exc_dev, 1, 1, 1, 1, 1, exc_dev)
    ones = np.ones((1, 1, 1, 8, 1, 1, 2, 1), np.float32)
    summing = (choose * part_eye * exc_eye * ones).reshape(2 * exc_dev * box_dev, -1)
    placed = jnp.dot(summing, result, precision=lax.Precision.HIGHEST)
    return placed.reshape(2, exc_dev, box_dev, V)


def encode(sources, enc_table):
    product = jnp.einsum(
        "ckv,xebv->ckxeb", enc_table, sources, preferred_element_type=jnp.float32
    )
    return jnp.stack(
        [product[0, :, 0] - product[1, :, 1], product[1, :, 0] + product[0, :, 1]], axis=1
    ).astype(jnp.bfloat16)


def translate(encoded, translators):
    product = jnp.einsum(
        "kcts,kxes->kcxet", translators, encoded, preferred_element_type=jnp.float32
    )
    return jnp.stack(
        [product[:, 0, 0] - product[:, 1, 1], product[:, 1, 0] + product[:, 0, 1]], axis=1
    ).astype(jnp.bfloat16)


def decode(returned, dec_table):
    product = jnp.einsum(
        "cvk,kxeb->cxebv", dec_table, returned, preferred_element_type=jnp.float32
    )
    return jnp.stack([product[0, 0] - product[1, 1], product[1, 0] + product[0, 1]])


def shards(incident, contrast, box_pos, directions, enc_table, dec_table):
    contrast_real = contrast.astype(jnp.float32) * chi_step
    translators = build_translators(directions, box_pos)
    fields = incident
    outputs = []
    for term_index in range(2):
        sources = (contrast_real[None, None] * fields.astype(jnp.float32)).astype(jnp.bfloat16)
        encoded = encode(sources, enc_table)
        translated = translate(
            lax.all_to_all(encoded, "box", split_axis=0, concat_axis=3, tiled=True), translators
        )
        sources, translated = lax.optimization_barrier((sources, translated))
        near_part = near_field(sources, box_pos)
        returned = lax.all_to_all(translated, "box", split_axis=3, concat_axis=0, tiled=True)
        fields = (near_part + decode(returned, dec_table)).astype(jnp.bfloat16)
        outputs.append(fields)
    first_sq = jnp.sum(jnp.square(outputs[0].astype(jnp.float32)), axis=(0, 1, 3))
    second_sq = jnp.sum(jnp.square(outputs[1].astype(jnp.float32)), axis=(0, 1, 3))
    first_sum, second_sum = lax.psum((first_sq, second_sq), "exc")
    entry_count = 2 * outputs[0].shape[1] * lax.axis_size("exc") * outputs[0].shape[3]
    series_ratio = jnp.sqrt(second_sum / entry_count / (first_sum / entry_count + epsilon))
    return (outputs[0], outputs[1], series_ratio)


def solution(mesh):
    placed = (P(None, "exc", "box", None), P("box", None), P(), P(None, "box"), P(), P())
    return jax.shard_map(
        shards,
        mesh=mesh,
        in_specs=placed,
        out_specs=(P(None, "exc", "box", None), P(None, "exc", "box", None), P("box")),
        check_vma=False,
    )
```
